128 devices in a mesh: gx: 32 (over y, x, core), gy: 4 (over z).
Axes of the slice: x: 4, y: 4, z: 4, core: 2. Of those that a mesh axis runs over, the one named last changes fastest.
Arguments:
- east_blocks: int32 [64, 4], P(None, 'gy'), may hold values from 0 to 2, as said below
- job_code: int32 [832, 4], P('gx', 'gy'), may hold values from -1 to 2282, as said below
- factor_panels: bfloat16 [832, 4, 2, 1536, 128], P('gx', 'gy'), as said below
- dual_rhs: float32 [64, 4, 256, 384], P('gx', 'gy'), may hold values from -6 to 6
Outputs:
- multipliers: float32 [64, 4, 256, 384], P('gx', 'gy')
- residual: float32 [64, 4, 256, 384], P('gx', 'gy')
The draws below stay inside these ranges and needn't reach their ends.
Inputs may be any that keep to these rules, and one draw needn't show every extreme that they name: `east_blocks`: in each row sy the faces sx = s0 to s0 + 15 carry 2 blocks, for a start s0 drawn per row from 1 to 46; the other faces carry 1, and the face at sx = 63 carries 0. `job_code`: A code (sx * 6 + bi) * 6 + bj names the upper tile bi <= bj < nb of subdomain (sx, sy) for column sy. In each column the live tiles, ordered by sx, then bi, then bj, are numbered k = 0, 1, ... and sit at row (k % 32) * 26 + k // 32; all other slots hold -1. Hence one device of gx forms at most 2 tiles of the subdomains of one gx index, and exactly 2 for some. `factor_panels`: A live slot holds column blocks bi and bj of subdomain (sx, sy)'s factor of 1536 rows and 768 columns, the same block wherever it appears; empty slots hold zeros.
All inputs are finite; a program needn't handle non-finite values.
Results may differ from the reference program's by a relative error of at most 0.0059.
Values may be sent and summed in bfloat16 or wider, within the bound.
No kernel may reach another device: no remote copies, remote signals or barrier semaphores. Data moves between devices by JAX's collectives and lax.ppermute only.
A program may use at most 128 MiB of HBM per device.

```python
from functools import partial
import jax
import jax.numpy as jnp
from jax import lax

NB = 6
BLK = 128
KF = 1536
CASES = 256
ITERS = 4
SX = 64
SY = 4
BANDF = 16
FACE = 384
JOB_DEV = 26
N_GX = 32


def band_starts(key):
    return jax.random.randint(jax.random.fold_in(key, 11), (SY,), 1, SX - 1 - BANDF).astype(jnp.int32)


def face_blocks(key):
    starts = band_starts(key)
    face_index = jnp.arange(SX, dtype=jnp.int32)[:, None]
    is_heavy = (face_index >= starts[None, :]) & (face_index < starts[None, :] + BANDF)
    blocks = jnp.where(is_heavy, 2, 1).astype(jnp.int32)
    return jnp.where(face_index < SX - 1, blocks, 0).astype(jnp.int32)


def tile_table(key):
    east_part = face_blocks(key)
    west_part = jnp.concatenate([jnp.zeros((1, SY), jnp.int32), east_part[:-1]], axis=0)
    row_index = jnp.arange(SY, dtype=jnp.int32)[None, :]
    interface_blocks = west_part + east_part + (row_index > 0).astype(jnp.int32) + (row_index < SY - 1).astype(jnp.int32)
    all_codes = jnp.arange(SX * NB * NB, dtype=jnp.int32)
    owner_sx = all_codes // (NB * NB)
    first_block = all_codes % (NB * NB) // NB
    second = all_codes % NB
    is_live = (first_block <= second)[:, None] & (second[:, None] < interface_blocks[owner_sx])
    tile_order = jnp.cumsum(is_live.astype(jnp.int32), axis=0) - 1
    place_slots = tile_order % N_GX * JOB_DEV + tile_order // N_GX
    place_slots = jnp.where(is_live, place_slots, N_GX * JOB_DEV).astype(jnp.int32)
    column_ids = jnp.broadcast_to(jnp.arange(SY, dtype=jnp.int32)[None, :], is_live.shape)
    values = jnp.broadcast_to(all_codes[:, None], is_live.shape)
    code_table = jnp.full((N_GX * JOB_DEV, SY), -1, jnp.int32)
    return code_table.at[place_slots, column_ids].set(values, mode='drop')


def draw_east_blocks(key, part):
    return face_blocks(key)


def draw_job_code(key, part):
    return tile_table(key)


def draw_factor_panels(key, part):
    code_table = tile_table(key).reshape(-1)
    column_ids = jnp.arange(code_table.shape[0], dtype=jnp.int32) % SY
    base_key = jax.random.fold_in(key, 29)

    def one_slot(job_item):
        tile_code, column = job_item
        safe_code = jnp.maximum(tile_code, 0)
        owner_sx = safe_code // (NB * NB)
        first_block = safe_code % (NB * NB) // NB
        second = safe_code % NB

        def make_panel(block_index):
            panel_key = jax.random.fold_in(base_key, (owner_sx * SY + column) * NB + block_index)
            values = jax.random.normal(panel_key, (KF, BLK), jnp.float32)
            return values * KF ** (-0.5)
        panel_pair = jnp.stack([make_panel(first_block), make_panel(second)])
        return jnp.where(tile_code >= 0, panel_pair, 0.0).astype(jnp.bfloat16)
    panels = lax.map(one_slot, (code_table, column_ids))
    return panels.reshape(N_GX * JOB_DEV, SY, 2, KF, BLK)


def level_of(own_key, shape, split, smallest, top_value):
    level = 1.0
    for axis_at, parts in split:
        heights = jax.random.uniform(jax.random.fold_in(jax.random.fold_in(own_key, 6), axis_at), (parts,), jnp.float32, smallest / len(split), top_value / len(split))
        level = level * jnp.repeat(jnp.exp(heights), shape[axis_at] // parts).reshape((-1,) + (1,) * (len(shape) - 1 - axis_at))
    return level


def centred(stream_key, extent, spread, reach, split=(), kind=jnp.bfloat16):
    values = jax.random.normal(stream_key, extent, jnp.float32) * spread
    if len(split) > 0:
        values = level_of(stream_key, extent, split, -0.22, 0.18) * values
    return jnp.clip(values, min=-reach, max=reach).astype(kind)


def setup_inputs(seed: int = 0) -> dict:
    arg_keys = jax.random.split(jax.random.key(seed), 5)
    return {
        "east_blocks": draw_east_blocks(jax.random.fold_in(arg_keys[4], 71), 0),
        "job_code": draw_job_code(jax.random.fold_in(arg_keys[4], 71), 0),
        "factor_panels": draw_factor_panels(jax.random.fold_in(arg_keys[4], 71), 0),
        "dual_rhs": centred(arg_keys[3], (SX, SY, CASES, FACE), 1.0, 6.0, ((0, 32), (1, 4)), jnp.float32),
    }


CHEB_LOW = 0.2
CHEB_HIGH = 7.0


def block_mask(count, blocks, block_len):
    lane_block = jnp.arange(blocks * block_len, dtype=jnp.int32) // block_len
    return (lane_block < count).astype(jnp.float32)


def place_slots(west_part, east_part, south_part, north_part, counts, block_len):
    local_vec = jnp.zeros((west_part.shape[0], NB * block_len), jnp.float32)
    anchor = jnp.zeros((), jnp.int32)
    local_vec = lax.dynamic_update_slice(local_vec, west_part * block_mask(counts[0], 2, block_len), (anchor, anchor))
    local_vec = lax.dynamic_update_slice(local_vec, east_part * block_mask(counts[1], 2, block_len), (anchor, counts[0] * block_len))
    local_vec = lax.dynamic_update_slice(local_vec, south_part * block_mask(counts[2], 1, block_len), (anchor, (counts[0] + counts[1]) * block_len))
    local_vec = lax.dynamic_update_slice(local_vec, north_part * block_mask(counts[3], 1, block_len), (anchor, (counts[0] + counts[1] + counts[2]) * block_len))
    return local_vec


def read_slots(local_vec, counts, block_len):
    west_part = local_vec[:, :2 * block_len] * block_mask(counts[0], 2, block_len)
    east_part = lax.dynamic_slice_in_dim(local_vec, counts[0] * block_len, 2 * block_len, 1) * block_mask(counts[1], 2, block_len)
    south_part = lax.dynamic_slice_in_dim(local_vec, (counts[0] + counts[1]) * block_len, block_len, 1) * block_mask(counts[2], 1, block_len)
    north_part = lax.dynamic_slice_in_dim(local_vec, (counts[0] + counts[1] + counts[2]) * block_len, block_len, 1) * block_mask(counts[3], 1, block_len)
    return west_part, east_part, south_part, north_part


def place_all(west_part, east_part, south_part, north_part, counts, block_len):
    return jax.vmap(partial(place_slots, block_len=block_len))(west_part, east_part, south_part, north_part, counts)


def read_all(local_vec, counts, block_len):
    return jax.vmap(partial(read_slots, block_len=block_len))(local_vec, counts)


def symmetric(upper_tiles):
    upper_f = upper_tiles.astype(jnp.float32)
    flipped = jnp.swapaxes(jnp.swapaxes(upper_f, 1, 2), 3, 4)
    block_row = jnp.arange(NB, dtype=jnp.int32)
    keep_upper = (block_row[:, None] <= block_row[None, :])[None, :, :, None, None]
    full_tiles = jnp.where(keep_upper, upper_f, flipped)
    full_width = NB * upper_tiles.shape[3]
    return full_tiles.transpose(0, 1, 3, 2, 4).reshape(upper_tiles.shape[0], full_width, full_width)


def face_mask(counts, block_len):
    east_lane = jnp.arange(2 * block_len, dtype=jnp.int32) // block_len
    east_ok = east_lane < counts[..., 1:2]
    north_ok = jnp.zeros((block_len,), jnp.int32) < counts[..., 3:4]
    return jnp.concatenate([east_ok, north_ok], axis=-1).astype(jnp.float32)


def subdomain_counts(east_blocks):
    west_blocks = jnp.concatenate([jnp.zeros((1, SY), jnp.int32), east_blocks[:-1]], axis=0)
    row_index = jnp.arange(SY, dtype=jnp.int32)
    south_blocks = jnp.broadcast_to((row_index > 0).astype(jnp.int32)[None, :], (SX, SY))
    north_blocks = jnp.broadcast_to((row_index < SY - 1).astype(jnp.int32)[None, :], (SX, SY))
    return jnp.stack([west_blocks, east_blocks, south_blocks, north_blocks], axis=-1)


def job_tiles(factor_panels):
    grouped = factor_panels.reshape((N_GX, JOB_DEV) + factor_panels.shape[1:])

    def tiles_of(panel_group):
        left_panel = panel_group[:, :, 0].astype(jnp.float32)
        right_panel = panel_group[:, :, 1].astype(jnp.float32)
        return jnp.einsum("jyka,jykb->jyab", left_panel, right_panel, precision=lax.Precision.HIGHEST).astype(jnp.bfloat16)

    return lax.map(tiles_of, grouped).reshape((N_GX * JOB_DEV, SY, BLK, BLK))


def flatten(array):
    return array.reshape((SX * SY,) + array.shape[2:])


def apply_global(face_vec, matrices, flat_counts):
    east_part = face_vec[..., :2 * BLK]
    north_part = face_vec[..., 2 * BLK:]
    from_west = jnp.concatenate([jnp.zeros_like(east_part[:1]), east_part[:-1]], axis=0)
    from_south = jnp.concatenate([jnp.zeros_like(north_part[:, :1]), north_part[:, :-1]], axis=1)
    local_vec = place_all(flatten(-from_west), flatten(east_part), flatten(-from_south), flatten(north_part), flat_counts, BLK)
    image = jnp.einsum("ncm,nmk->nck", local_vec, matrices, precision=lax.Precision.HIGHEST)
    west_y, east_y, south_y, north_y = read_all(image, flat_counts, BLK)
    west_y = west_y.reshape(SX, SY, CASES, 2 * BLK)
    east_y = east_y.reshape(SX, SY, CASES, 2 * BLK)
    south_y = south_y.reshape(SX, SY, CASES, BLK)
    north_y = north_y.reshape(SX, SY, CASES, BLK)
    east_near = jnp.concatenate([west_y[1:], jnp.zeros_like(west_y[:1])], axis=0)
    north_near = jnp.concatenate([south_y[:, 1:], jnp.zeros_like(south_y[:, :1])], axis=1)
    return jnp.concatenate([east_y - east_near, north_y - north_near], axis=-1)


def reference(east_blocks, job_code, factor_panels, dual_rhs):
    counts = subdomain_counts(east_blocks)
    flat_counts = counts.reshape(SX * SY, 4)
    tiles = job_tiles(factor_panels)
    column_ids = jnp.broadcast_to(jnp.arange(SY, dtype=jnp.int32)[None, :], job_code.shape)
    target = jnp.where(job_code >= 0, job_code, SX * NB * NB).astype(jnp.int32)
    upper_tiles = jnp.zeros((SX * NB * NB, SY, BLK, BLK), jnp.bfloat16).at[target, column_ids].set(tiles, mode="drop")
    upper_tiles = upper_tiles.reshape(SX, NB, NB, SY, BLK, BLK).transpose(0, 3, 1, 2, 4, 5).reshape(SX * SY, NB, NB, BLK, BLK)
    matrices = lax.map(lambda single: symmetric(single[None])[0], upper_tiles)
    face_ok = face_mask(counts, BLK)[:, :, None, :]
    residual = dual_rhs * face_ok
    cheb_center = (CHEB_HIGH + CHEB_LOW) / 2.0
    cheb_radius = (CHEB_HIGH - CHEB_LOW) / 2.0
    cheb_ratio = cheb_center / cheb_radius
    cheb_rho = 1.0 / cheb_ratio
    update = residual / cheb_center
    multipliers = jnp.zeros_like(residual)
    for sweep in range(ITERS):
        multipliers = multipliers + update
        residual = residual - apply_global(update, matrices, flat_counts)
        rho_next = 1.0 / (2.0 * cheb_ratio - cheb_rho)
        update = (rho_next * cheb_rho) * update + (2.0 * rho_next / cheb_radius) * residual
        cheb_rho = rho_next
    return multipliers, residual
```

```python
import jax
import jax.numpy as jnp
from jax import lax
from jax.sharding import PartitionSpec as P

NB = 6
ITERS = 4


CHEB_LOW = 0.2
CHEB_HIGH = 7.0


def from_behind(value, axis, steps):
    count = lax.axis_size(axis)
    initial, last = (max(0, -steps), min(count, count - steps))
    return lax.ppermute(value, axis, [(source, source + steps) for source in range(initial, last)])


def face_mask(counts, block_len):
    east_lane = jnp.arange(2 * block_len, dtype=jnp.int32) // block_len
    east_ok = east_lane < counts[..., 1:2]
    north_ok = jnp.zeros((block_len,), jnp.int32) < counts[..., 3:4]
    return jnp.concatenate([east_ok, north_ok], axis=-1).astype(jnp.float32)


def logical_slots(counts):
    west_n = counts[:, 0:1]
    east_n = counts[:, 1:2]
    south_n = counts[:, 2:3]
    north_n = counts[:, 3:4]
    within = jnp.array([0, 1, 0, 1, 0, 0], jnp.int32)[None, :]
    zero = jnp.zeros_like(west_n)
    offsets = jnp.concatenate(
        [zero, zero, west_n, west_n, west_n + east_n, west_n + east_n + south_n], axis=1
    )
    limits = jnp.concatenate([west_n, west_n, east_n, east_n, south_n, north_n], axis=1)
    return offsets + within, within < limits


def shards(east_blocks, job_code, factor_panels, dual_rhs):
    gx_count = lax.axis_size("gx")
    gy_count = lax.axis_size("gy")
    gx_index = lax.axis_index("gx")
    gy_index = lax.axis_index("gy")
    block_len = factor_panels.shape[-1]
    sub_count = dual_rhs.shape[0]
    column = east_blocks[:, 0]
    west_column = jnp.concatenate([jnp.zeros((1,), jnp.int32), column[:-1]])
    south_one = (gy_index > 0).astype(jnp.int32)
    north_one = (gy_index < gy_count - 1).astype(jnp.int32)
    blocks_all = west_column + column + south_one + north_one
    tiles_all = blocks_all * (blocks_all + 1) // 2
    first_tile_all = jnp.cumsum(tiles_all) - tiles_all
    first_sub = gx_index * sub_count
    east_own = lax.dynamic_slice_in_dim(column, first_sub, sub_count)
    west_own = lax.dynamic_slice_in_dim(west_column, first_sub, sub_count)
    blocks_own = lax.dynamic_slice_in_dim(blocks_all, first_sub, sub_count)
    first_tile_own = lax.dynamic_slice_in_dim(first_tile_all, first_sub, sub_count)
    south_own = jnp.broadcast_to(south_one, (sub_count,))
    north_own = jnp.broadcast_to(north_one, (sub_count,))
    counts = jnp.stack([west_own, east_own, south_own, north_own], axis=-1)

    tiles = jnp.einsum(
        "jka,jkb->jab",
        factor_panels[:, 0, 0],
        factor_panels[:, 0, 1],
        preferred_element_type=jnp.float32,
    ).astype(jnp.bfloat16)
    tile_codes = job_code[:, 0]
    job_count = tile_codes.shape[0]
    is_valid = tile_codes >= 0
    owner_gx = jnp.where(is_valid, tile_codes // (NB * NB) // sub_count, 0)
    slot_cap = (sub_count * NB * (NB + 1) // 2 + gx_count - 1) // gx_count
    job_order = jnp.arange(job_count, dtype=jnp.int32)
    same_owner = (
        (owner_gx[:, None] == owner_gx[None, :])
        & is_valid[None, :]
        & (job_order[None, :] < job_order[:, None])
    )
    slot_rank = jnp.sum(same_owner.astype(jnp.int32), axis=1)
    send_slot = jnp.where(is_valid & (slot_rank < slot_cap), owner_gx * slot_cap + slot_rank, -1)
    slot_count = gx_count * slot_cap
    pick_send = (
        send_slot[None, :] == jnp.arange(slot_count, dtype=jnp.int32)[:, None]
    ).astype(jnp.bfloat16)
    send_tiles = jnp.einsum(
        "mj,jab->mab", pick_send, tiles, preferred_element_type=jnp.float32
    ).astype(jnp.bfloat16)
    send_tiles = send_tiles.reshape(gx_count, slot_cap, block_len, block_len)
    got_tiles = lax.all_to_all(send_tiles, "gx", split_axis=0, concat_axis=0, tiled=True)
    got_tiles = got_tiles.reshape(slot_count, block_len, block_len)

    source, alive = logical_slots(counts)
    row_slot = source[:, :, None]
    col_slot = source[:, None, :]
    low_slot = jnp.minimum(row_slot, col_slot)
    high_slot = jnp.maximum(row_slot, col_slot)
    nb = blocks_own[:, None, None]
    pair_index = low_slot * nb - low_slot * (low_slot - 1) // 2 + (high_slot - low_slot)
    tile_number = first_tile_own[:, None, None] + pair_index
    local_number = tile_number - first_tile_own[0]
    got_slot = tile_number % gx_count * slot_cap + local_number // gx_count
    both_alive = alive[:, :, None] & alive[:, None, :]
    slot_ids = jnp.arange(slot_count, dtype=jnp.int32)
    hits = got_slot[..., None] == slot_ids
    pick_upper = (hits & (both_alive & (row_slot <= col_slot))[..., None]).astype(jnp.bfloat16)
    pick_lower = (hits & (both_alive & (row_slot > col_slot))[..., None]).astype(jnp.bfloat16)
    matrices = jnp.einsum(
        "spqf,fab->spaqb", pick_upper, got_tiles, preferred_element_type=jnp.float32
    ) + jnp.einsum(
        "spqf,fba->spaqb", pick_lower, got_tiles, preferred_element_type=jnp.float32
    )
    matrices = matrices.astype(jnp.bfloat16).reshape(sub_count, NB * block_len, NB * block_len)

    residual = dual_rhs[:, 0] * face_mask(counts, block_len)[:, None, :]
    cases = residual.shape[1]
    cheb_center = (CHEB_HIGH + CHEB_LOW) / 2.0
    cheb_radius = (CHEB_HIGH - CHEB_LOW) / 2.0
    cheb_ratio = cheb_center / cheb_radius
    cheb_rho = 1.0 / cheb_ratio
    update = residual / cheb_center
    multipliers = jnp.zeros_like(residual)
    for sweep in range(ITERS):
        multipliers = multipliers + update
        east_part = update[..., : 2 * block_len]
        to_north_part = update[..., 2 * block_len :]
        from_west = from_behind(east_part[sub_count - 1], "gx", 1)
        from_south = from_behind(to_north_part, "gy", 1)
        west_in = -jnp.concatenate([from_west[None], east_part[: sub_count - 1]], axis=0)
        local_vec = jnp.concatenate([west_in, east_part, -from_south, to_north_part], axis=-1)
        high = local_vec.astype(jnp.bfloat16)
        low = (local_vec - high.astype(jnp.float32)).astype(jnp.bfloat16)
        both = jnp.einsum(
            "ncm,nmk->nck",
            jnp.concatenate([high, low], axis=1),
            matrices,
            preferred_element_type=jnp.float32,
        )
        image = both[:, :cases] + both[:, cases:]
        west_part = image[..., : 2 * block_len]
        split_east_part = image[..., 2 * block_len : 4 * block_len]
        south_part = image[..., 4 * block_len : 5 * block_len]
        split_north_part = image[..., 5 * block_len :]
        from_east = from_behind(west_part[0], "gx", -1)
        from_north = from_behind(south_part, "gy", -1)
        east_near = jnp.concatenate([west_part[1:], from_east[None]], axis=0)
        residual = residual - jnp.concatenate(
            [split_east_part - east_near, split_north_part - from_north], axis=-1
        )
        rho_next = 1.0 / (2.0 * cheb_ratio - cheb_rho)
        update = rho_next * cheb_rho * update + 2.0 * rho_next / cheb_radius * residual
        cheb_rho = rho_next
    return (multipliers[:, None], residual[:, None])


def solution(mesh):
    in_specs = (
        P(None, "gy"),
        P("gx", "gy"),
        P("gx", "gy", None, None, None),
        P("gx", "gy", None, None),
    )
    out_specs = (P("gx", "gy", None, None), P("gx", "gy", None, None))
    return jax.shard_map(shards, mesh=mesh, in_specs=in_specs, out_specs=out_specs, check_vma=False)
```

```python
import jax
import jax.numpy as jnp
from jax import lax
from jax.sharding import PartitionSpec as P

NB = 6
ITERS = 4


CHEB_LOW = 0.2
CHEB_HIGH = 7.0


def from_behind(value, axis, steps):
    count = lax.axis_size(axis)
    initial, last = (max(0, -steps), min(count, count - steps))
    return lax.ppermute(value, axis, [(source, source + steps) for source in range(initial, last)])


def face_mask(counts, block_len):
    east_lane = jnp.arange(2 * block_len, dtype=jnp.int32) // block_len
    east_ok = east_lane < counts[..., 1:2]
    north_ok = jnp.zeros((block_len,), jnp.int32) < counts[..., 3:4]
    return jnp.concatenate([east_ok, north_ok], axis=-1).astype(jnp.float32)


def logical_slots(counts):
    west_n = counts[:, 0:1]
    east_n = counts[:, 1:2]
    south_n = counts[:, 2:3]
    north_n = counts[:, 3:4]
    within = jnp.array([0, 1, 0, 1, 0, 0], jnp.int32)[None, :]
    zero = jnp.zeros_like(west_n)
    offsets = jnp.concatenate(
        [zero, zero, west_n, west_n, west_n + east_n, west_n + east_n + south_n], axis=1
    )
    limits = jnp.concatenate([west_n, west_n, east_n, east_n, south_n, north_n], axis=1)
    return offsets + within, within < limits


def shards(east_blocks, job_code, factor_panels, dual_rhs):
    gx_count = lax.axis_size("gx")
    gy_count = lax.axis_size("gy")
    gx_index = lax.axis_index("gx")
    gy_index = lax.axis_index("gy")
    block_len = factor_panels.shape[-1]
    sub_count = dual_rhs.shape[0]
    column = east_blocks[:, 0]
    west_column = jnp.concatenate([jnp.zeros((1,), jnp.int32), column[:-1]])
    south_one = (gy_index > 0).astype(jnp.int32)
    north_one = (gy_index < gy_count - 1).astype(jnp.int32)
    blocks_all = west_column + column + south_one + north_one
    tiles_all = blocks_all * (blocks_all + 1) // 2
    first_tile_all = jnp.cumsum(tiles_all) - tiles_all
    first_sub = gx_index * sub_count
    east_own = lax.dynamic_slice_in_dim(column, first_sub, sub_count)
    west_own = lax.dynamic_slice_in_dim(west_column, first_sub, sub_count)
    blocks_own = lax.dynamic_slice_in_dim(blocks_all, first_sub, sub_count)
    first_tile_own = lax.dynamic_slice_in_dim(first_tile_all, first_sub, sub_count)
    south_own = jnp.broadcast_to(south_one, (sub_count,))
    north_own = jnp.broadcast_to(north_one, (sub_count,))
    counts = jnp.stack([west_own, east_own, south_own, north_own], axis=-1)

    tiles = jnp.einsum(
        "jka,jkb->jab",
        factor_panels[:, 0, 0],
        factor_panels[:, 0, 1],
        preferred_element_type=jnp.float32,
    ).astype(jnp.bfloat16)
    tile_codes = job_code[:, 0]
    job_count = tile_codes.shape[0]
    is_valid = tile_codes >= 0
    owner_gx = jnp.where(is_valid, tile_codes // (NB * NB) // sub_count, 0)
    slot_cap = (sub_count * NB * (NB + 1) // 2 + gx_count - 1) // gx_count
    job_order = jnp.arange(job_count, dtype=jnp.int32)
    same_owner = (
        (owner_gx[:, None] == owner_gx[None, :])
        & is_valid[None, :]
        & (job_order[None, :] < job_order[:, None])
    )
    slot_rank = jnp.sum(same_owner.astype(jnp.int32), axis=1)
    send_slot = jnp.where(is_valid & (slot_rank < slot_cap), owner_gx * slot_cap + slot_rank, -1)
    slot_count = gx_count * slot_cap
    pick_send = (
        send_slot[None, :] == jnp.arange(slot_count, dtype=jnp.int32)[:, None]
    ).astype(jnp.bfloat16)
    send_tiles = jnp.einsum(
        "mj,jab->mab", pick_send, tiles, preferred_element_type=jnp.float32
    ).astype(jnp.bfloat16)
    send_tiles = send_tiles.reshape(gx_count, slot_cap * block_len, block_len)
    got_tiles = lax.all_to_all(send_tiles, "gx", split_axis=0, concat_axis=0, tiled=True)
    got_tiles = got_tiles.reshape(slot_count, block_len, block_len)

    source, alive = logical_slots(counts)
    row_slot = source[:, :, None]
    col_slot = source[:, None, :]
    low_slot = jnp.minimum(row_slot, col_slot)
    high_slot = jnp.maximum(row_slot, col_slot)
    nb = blocks_own[:, None, None]
    pair_index = low_slot * nb - low_slot * (low_slot - 1) // 2 + (high_slot - low_slot)
    tile_number = first_tile_own[:, None, None] + pair_index
    local_number = tile_number - first_tile_own[0]
    got_slot = tile_number % gx_count * slot_cap + local_number // gx_count
    both_alive = alive[:, :, None] & alive[:, None, :]
    slot_ids = jnp.arange(slot_count, dtype=jnp.int32)
    hits = got_slot[..., None] == slot_ids
    pick_upper = (hits & (both_alive & (row_slot <= col_slot))[..., None]).astype(jnp.bfloat16)
    pick_lower = (hits & (both_alive & (row_slot > col_slot))[..., None]).astype(jnp.bfloat16)
    matrices = jnp.einsum(
        "spqf,fab->spaqb", pick_upper, got_tiles, preferred_element_type=jnp.float32
    ) + jnp.einsum(
        "spqf,fba->spaqb", pick_lower, got_tiles, preferred_element_type=jnp.float32
    )
    matrices = matrices.astype(jnp.bfloat16).reshape(sub_count, NB * block_len, NB * block_len)

    residual = dual_rhs[:, 0] * face_mask(counts, block_len)[:, None, :]
    cases = residual.shape[1]
    cheb_center = (CHEB_HIGH + CHEB_LOW) / 2.0
    cheb_radius = (CHEB_HIGH - CHEB_LOW) / 2.0
    cheb_ratio = cheb_center / cheb_radius
    cheb_rho = 1.0 / cheb_ratio
    west_residual = from_behind(residual[sub_count - 1, :, : 2 * block_len], "gx", 1)
    south_residual = from_behind(residual[..., 2 * block_len :], "gy", 1)
    update = residual / cheb_center
    west_update = west_residual / cheb_center
    south_update = south_residual / cheb_center
    multipliers = jnp.zeros_like(residual)
    for sweep in range(ITERS):
        multipliers = multipliers + update
        east_part = update[..., : 2 * block_len]
        to_north_part = update[..., 2 * block_len :]
        west_in = -jnp.concatenate([west_update[None], east_part[: sub_count - 1]], axis=0)
        local_vec = jnp.concatenate([west_in, east_part, -south_update, to_north_part], axis=-1)
        high_f = lax.reduce_precision(local_vec, exponent_bits=8, mantissa_bits=7)
        high = high_f.astype(jnp.bfloat16)
        low = (local_vec - high_f).astype(jnp.bfloat16)
        both = jnp.einsum(
            "ncm,nmk->nck",
            jnp.concatenate([high, low], axis=1),
            matrices,
            preferred_element_type=jnp.float32,
        )
        image = both[:, :cases] + both[:, cases:]
        west_part = image[..., : 2 * block_len]
        split_east_part = image[..., 2 * block_len : 4 * block_len]
        south_part = image[..., 4 * block_len : 5 * block_len]
        split_north_part = image[..., 5 * block_len :]
        from_east = from_behind(west_part[0], "gx", -1)
        from_north = from_behind(south_part, "gy", -1)
        last = sweep == ITERS - 1
        if not last:
            west_east_part = from_behind(split_east_part[sub_count - 1], "gx", 1)
            south_north_part = from_behind(split_north_part, "gy", 1)
        east_near = jnp.concatenate([west_part[1:], from_east[None]], axis=0)
        residual = residual - jnp.concatenate(
            [split_east_part - east_near, split_north_part - from_north], axis=-1
        )
        rho_next = 1.0 / (2.0 * cheb_ratio - cheb_rho)
        keep = rho_next * cheb_rho
        step = 2.0 * rho_next / cheb_radius
        update = keep * update + step * residual
        if not last:
            west_residual = west_residual - (west_east_part - west_part[0])
            south_residual = south_residual - (south_north_part - south_part)
            west_update = keep * west_update + step * west_residual
            south_update = keep * south_update + step * south_residual
        cheb_rho = rho_next
    return (multipliers[:, None], residual[:, None])


def solution(mesh):
    in_specs = (
        P(None, "gy"),
        P("gx", "gy"),
        P("gx", "gy", None, None, None),
        P("gx", "gy", None, None),
    )
    out_specs = (P("gx", "gy", None, None), P("gx", "gy", None, None))
    return jax.shard_map(shards, mesh=mesh, in_specs=in_specs, out_specs=out_specs, check_vma=False)
```

```python
from functools import partial

import jax
import jax.numpy as jnp
from jax import lax
from jax.experimental import pallas as pl
from jax.experimental.pallas import tpu as pltpu
from jax.sharding import PartitionSpec as P

NB = 6
ITERS = 4


CHEB_LOW = 0.2
CHEB_HIGH = 7.0


def from_behind(value, axis, steps):
    count = lax.axis_size(axis)
    initial, last = (max(0, -steps), min(count, count - steps))
    return lax.ppermute(value, axis, [(source, source + steps) for source in range(initial, last)])


def _gather_kernel(table_ref, tiles_ref, out_ref, *, rows, cols, block_len):
    for r in range(rows):
        for c in range(cols):
            entry = r * cols + c
            index = table_ref[0, entry]
            mode = table_ref[1, entry]
            rs = slice(r * block_len, (r + 1) * block_len)
            cs = slice(c * block_len, (c + 1) * block_len)

            @pl.when(mode == 0)
            def _():
                out_ref[rs, cs] = jnp.zeros((block_len, block_len), out_ref.dtype)

            @pl.when(mode == 1)
            def _():
                out_ref[rs, cs] = tiles_ref[index]

            @pl.when(mode == 2)
            def _():
                out_ref[rs, cs] = tiles_ref[index].astype(jnp.float32).T.astype(out_ref.dtype)


def gather_tiles(table, tiles, rows, cols):
    block_len = tiles.shape[-1]
    count = tiles.shape[0]
    kernel = partial(_gather_kernel, rows=rows, cols=cols, block_len=block_len)
    size = 2 * block_len * block_len
    return pl.pallas_call(
        kernel,
        out_shape=jax.ShapeDtypeStruct((rows * block_len, cols * block_len), tiles.dtype),
        in_specs=[
            pl.BlockSpec(memory_space=pltpu.SMEM),
            pl.BlockSpec(memory_space=pltpu.VMEM),
        ],
        out_specs=pl.BlockSpec(memory_space=pltpu.VMEM),
        cost_estimate=pl.CostEstimate(
            flops=0, transcendentals=0, bytes_accessed=(count + rows * cols) * size
        ),
    )(table, tiles)


def face_mask(counts, block_len):
    east_lane = jnp.arange(2 * block_len, dtype=jnp.int32) // block_len
    east_ok = east_lane < counts[..., 1:2]
    north_ok = jnp.zeros((block_len,), jnp.int32) < counts[..., 3:4]
    return jnp.concatenate([east_ok, north_ok], axis=-1).astype(jnp.float32)


def logical_slots(counts):
    west_n = counts[:, 0:1]
    east_n = counts[:, 1:2]
    south_n = counts[:, 2:3]
    north_n = counts[:, 3:4]
    within = jnp.array([0, 1, 0, 1, 0, 0], jnp.int32)[None, :]
    zero = jnp.zeros_like(west_n)
    offsets = jnp.concatenate(
        [zero, zero, west_n, west_n, west_n + east_n, west_n + east_n + south_n], axis=1
    )
    limits = jnp.concatenate([west_n, west_n, east_n, east_n, south_n, north_n], axis=1)
    return offsets + within, within < limits


def shards(east_blocks, job_code, factor_panels, dual_rhs):
    gx_count = lax.axis_size("gx")
    gy_count = lax.axis_size("gy")
    gx_index = lax.axis_index("gx")
    gy_index = lax.axis_index("gy")
    block_len = factor_panels.shape[-1]
    sub_count = dual_rhs.shape[0]
    column = east_blocks[:, 0]
    west_column = jnp.concatenate([jnp.zeros((1,), jnp.int32), column[:-1]])
    south_one = (gy_index > 0).astype(jnp.int32)
    north_one = (gy_index < gy_count - 1).astype(jnp.int32)
    blocks_all = west_column + column + south_one + north_one
    tiles_all = blocks_all * (blocks_all + 1) // 2
    first_tile_all = jnp.cumsum(tiles_all) - tiles_all
    first_sub = gx_index * sub_count
    east_own = lax.dynamic_slice_in_dim(column, first_sub, sub_count)
    west_own = lax.dynamic_slice_in_dim(west_column, first_sub, sub_count)
    blocks_own = lax.dynamic_slice_in_dim(blocks_all, first_sub, sub_count)
    first_tile_own = lax.dynamic_slice_in_dim(first_tile_all, first_sub, sub_count)
    south_own = jnp.broadcast_to(south_one, (sub_count,))
    north_own = jnp.broadcast_to(north_one, (sub_count,))
    counts = jnp.stack([west_own, east_own, south_own, north_own], axis=-1)

    tiles = jnp.einsum(
        "jka,jkb->jab",
        factor_panels[:, 0, 0],
        factor_panels[:, 0, 1],
        preferred_element_type=jnp.float32,
    ).astype(jnp.bfloat16)
    tile_codes = job_code[:, 0]
    job_count = tile_codes.shape[0]
    is_valid = tile_codes >= 0
    owner_gx = jnp.where(is_valid, tile_codes // (NB * NB) // sub_count, 0)
    slot_cap = (sub_count * NB * (NB + 1) // 2 + gx_count - 1) // gx_count
    job_order = jnp.arange(job_count, dtype=jnp.int32)
    same_owner = (
        (owner_gx[:, None] == owner_gx[None, :])
        & is_valid[None, :]
        & (job_order[None, :] < job_order[:, None])
    )
    slot_rank = jnp.sum(same_owner.astype(jnp.int32), axis=1)
    send_slot = jnp.where(is_valid & (slot_rank < slot_cap), owner_gx * slot_cap + slot_rank, -1)
    slot_count = gx_count * slot_cap
    send_hit = send_slot[None, :] == jnp.arange(slot_count, dtype=jnp.int32)[:, None]
    send_from = jnp.sum(jnp.where(send_hit, job_order[None, :], 0), axis=1)
    send_mode = jnp.any(send_hit, axis=1).astype(jnp.int32)
    send_tiles = gather_tiles(jnp.stack([send_from, send_mode]), tiles, slot_count, 1)
    send_tiles = send_tiles.reshape(gx_count, slot_cap * block_len, block_len)
    got_tiles = lax.all_to_all(send_tiles, "gx", split_axis=0, concat_axis=0, tiled=True)
    got_tiles = got_tiles.reshape(slot_count, block_len, block_len)

    source, alive = logical_slots(counts)
    row_slot = source[:, :, None]
    col_slot = source[:, None, :]
    low_slot = jnp.minimum(row_slot, col_slot)
    high_slot = jnp.maximum(row_slot, col_slot)
    nb = blocks_own[:, None, None]
    pair_index = low_slot * nb - low_slot * (low_slot - 1) // 2 + (high_slot - low_slot)
    tile_number = first_tile_own[:, None, None] + pair_index
    local_number = tile_number - first_tile_own[0]
    got_slot = tile_number % gx_count * slot_cap + local_number // gx_count
    both_alive = alive[:, :, None] & alive[:, None, :]
    matrix_mode = jnp.where(both_alive, jnp.where(row_slot <= col_slot, 1, 2), 0)
    matrix_from = jnp.where(both_alive, jnp.clip(got_slot, 0, slot_count - 1), 0)
    matrices = jnp.stack(
        [
            gather_tiles(
                jnp.stack([matrix_from[sub].reshape(-1), matrix_mode[sub].reshape(-1)]),
                got_tiles,
                NB,
                NB,
            )
            for sub in range(sub_count)
        ]
    )

    residual = dual_rhs[:, 0] * face_mask(counts, block_len)[:, None, :]
    cases = residual.shape[1]
    cheb_center = (CHEB_HIGH + CHEB_LOW) / 2.0
    cheb_radius = (CHEB_HIGH - CHEB_LOW) / 2.0
    cheb_ratio = cheb_center / cheb_radius
    cheb_rho = 1.0 / cheb_ratio
    west_residual = from_behind(residual[sub_count - 1, :, : 2 * block_len], "gx", 1)
    south_residual = from_behind(residual[..., 2 * block_len :], "gy", 1)
    update = residual / cheb_center
    west_update = west_residual / cheb_center
    south_update = south_residual / cheb_center
    multipliers = jnp.zeros_like(residual)
    for sweep in range(ITERS):
        multipliers = multipliers + update
        east_part = update[..., : 2 * block_len]
        to_north_part = update[..., 2 * block_len :]
        west_in = -jnp.concatenate([west_update[None], east_part[: sub_count - 1]], axis=0)
        local_vec = jnp.concatenate([west_in, east_part, -south_update, to_north_part], axis=-1)
        high_f = lax.reduce_precision(local_vec, exponent_bits=8, mantissa_bits=7)
        high = high_f.astype(jnp.bfloat16)
        low = (local_vec - high_f).astype(jnp.bfloat16)
        both = jnp.einsum(
            "ncm,nmk->nck",
            jnp.concatenate([high, low], axis=1),
            matrices,
            preferred_element_type=jnp.float32,
        )
        image = both[:, :cases] + both[:, cases:]
        west_part = image[..., : 2 * block_len]
        split_east_part = image[..., 2 * block_len : 4 * block_len]
        south_part = image[..., 4 * block_len : 5 * block_len]
        split_north_part = image[..., 5 * block_len :]
        from_east = from_behind(west_part[0], "gx", -1)
        from_north = from_behind(south_part, "gy", -1)
        last = sweep == ITERS - 1
        if not last:
            west_east_part = from_behind(split_east_part[sub_count - 1], "gx", 1)
            south_north_part = from_behind(split_north_part, "gy", 1)
        east_near = jnp.concatenate([west_part[1:], from_east[None]], axis=0)
        residual = residual - jnp.concatenate(
            [split_east_part - east_near, split_north_part - from_north], axis=-1
        )
        rho_next = 1.0 / (2.0 * cheb_ratio - cheb_rho)
        keep = rho_next * cheb_rho
        step = 2.0 * rho_next / cheb_radius
        update = keep * update + step * residual
        if not last:
            west_residual = west_residual - (west_east_part - west_part[0])
            south_residual = south_residual - (south_north_part - south_part)
            west_update = keep * west_update + step * west_residual
            south_update = keep * south_update + step * south_residual
        cheb_rho = rho_next
    return (multipliers[:, None], residual[:, None])


def solution(mesh):
    in_specs = (
        P(None, "gy"),
        P("gx", "gy"),
        P("gx", "gy", None, None, None),
        P("gx", "gy", None, None),
    )
    out_specs = (P("gx", "gy", None, None), P("gx", "gy", None, None))
    return jax.shard_map(shards, mesh=mesh, in_specs=in_specs, out_specs=out_specs, check_vma=False)
```

```python
from functools import partial

import jax
import jax.numpy as jnp
from jax import lax
from jax.experimental import pallas as pl
from jax.experimental.pallas import tpu as pltpu
from jax.sharding import PartitionSpec as P

NB = 6
ITERS = 4


CHEB_LOW = 0.2
CHEB_HIGH = 7.0


def from_behind(value, axis, steps):
    count = lax.axis_size(axis)
    initial, last = (max(0, -steps), min(count, count - steps))
    return lax.ppermute(value, axis, [(source, source + steps) for source in range(initial, last)])


def _tile_kernel(dest_ref, panels_ref, out_ref, *, per_step, block_len):
    step = pl.program_id(0)

    @pl.when(step == 0)
    def _():
        out_ref[...] = jnp.zeros_like(out_ref)

    for u in range(per_step):
        slot = dest_ref[step * per_step + u]
        tile = lax.dot_general(
            panels_ref[u, 0, 0],
            panels_ref[u, 0, 1],
            (((0,), (0,)), ((), ())),
            preferred_element_type=jnp.float32,
        ).astype(out_ref.dtype)

        @pl.when(slot >= 0)
        def _():
            out_ref[pl.ds(pl.multiple_of(slot * block_len, block_len), block_len), :] = tile


def tiles_packed(dest, factor_panels, slot_count):
    job_count, _, _, rows, block_len = factor_panels.shape
    per_step = 2 if job_count % 2 == 0 else 1
    return pl.pallas_call(
        partial(_tile_kernel, per_step=per_step, block_len=block_len),
        out_shape=jax.ShapeDtypeStruct((slot_count * block_len, block_len), factor_panels.dtype),
        grid_spec=pltpu.PrefetchScalarGridSpec(
            num_scalar_prefetch=1,
            grid=(job_count // per_step,),
            in_specs=[
                pl.BlockSpec((per_step, 1, 2, rows, block_len), lambda i, dest: (i, 0, 0, 0, 0)),
            ],
            out_specs=pl.BlockSpec((slot_count * block_len, block_len), lambda i, dest: (0, 0)),
        ),
        cost_estimate=pl.CostEstimate(
            flops=2 * job_count * rows * block_len * block_len,
            transcendentals=0,
            bytes_accessed=factor_panels.size * 2 + slot_count * block_len * block_len * 2,
        ),
    )(dest, factor_panels)


def _matrix_kernel(table_ref, tiles_ref, out_ref, *, subs, blocks, block_len):
    for s in range(subs):
        for p in range(blocks):
            for q in range(p, blocks):
                entry = (s * blocks + p) * blocks + q
                tile = tiles_ref[table_ref[0, entry]]
                keep = table_ref[1, entry] != 0
                tile = jnp.where(keep, tile, jnp.zeros_like(tile))
                out_ref[s, p * block_len : (p + 1) * block_len, q * block_len : (q + 1) * block_len] = tile
                if q > p:
                    out_ref[s, q * block_len : (q + 1) * block_len, p * block_len : (p + 1) * block_len] = (
                        tile.astype(jnp.float32).T.astype(tile.dtype)
                    )


def matrix_tiles(table, tiles, subs, blocks):
    block_len = tiles.shape[-1]
    size = 2 * block_len * block_len
    width = blocks * block_len
    return pl.pallas_call(
        partial(_matrix_kernel, subs=subs, blocks=blocks, block_len=block_len),
        out_shape=jax.ShapeDtypeStruct((subs, width, width), tiles.dtype),
        in_specs=[
            pl.BlockSpec(memory_space=pltpu.SMEM),
            pl.BlockSpec(memory_space=pltpu.VMEM),
        ],
        out_specs=pl.BlockSpec(memory_space=pltpu.VMEM),
        cost_estimate=pl.CostEstimate(
            flops=0, transcendentals=0, bytes_accessed=(tiles.shape[0] + subs * blocks * blocks) * size
        ),
    )(table, tiles)


def face_mask(counts, block_len):
    east_lane = jnp.arange(2 * block_len, dtype=jnp.int32) // block_len
    east_ok = east_lane < counts[..., 1:2]
    north_ok = jnp.zeros((block_len,), jnp.int32) < counts[..., 3:4]
    return jnp.concatenate([east_ok, north_ok], axis=-1).astype(jnp.float32)


def logical_slots(counts):
    west_n = counts[:, 0:1]
    east_n = counts[:, 1:2]
    south_n = counts[:, 2:3]
    north_n = counts[:, 3:4]
    within = jnp.array([0, 1, 0, 1, 0, 0], jnp.int32)[None, :]
    zero = jnp.zeros_like(west_n)
    offsets = jnp.concatenate(
        [zero, zero, west_n, west_n, west_n + east_n, west_n + east_n + south_n], axis=1
    )
    limits = jnp.concatenate([west_n, west_n, east_n, east_n, south_n, north_n], axis=1)
    return offsets + within, within < limits


def shards(east_blocks, job_code, factor_panels, dual_rhs):
    gx_count = lax.axis_size("gx")
    gy_count = lax.axis_size("gy")
    gx_index = lax.axis_index("gx")
    gy_index = lax.axis_index("gy")
    block_len = factor_panels.shape[-1]
    sub_count = dual_rhs.shape[0]
    column = east_blocks[:, 0]
    west_column = jnp.concatenate([jnp.zeros((1,), jnp.int32), column[:-1]])
    south_one = (gy_index > 0).astype(jnp.int32)
    north_one = (gy_index < gy_count - 1).astype(jnp.int32)
    blocks_all = west_column + column + south_one + north_one
    tiles_all = blocks_all * (blocks_all + 1) // 2
    first_tile_all = jnp.cumsum(tiles_all) - tiles_all
    first_sub = gx_index * sub_count
    east_own = lax.dynamic_slice_in_dim(column, first_sub, sub_count)
    west_own = lax.dynamic_slice_in_dim(west_column, first_sub, sub_count)
    blocks_own = lax.dynamic_slice_in_dim(blocks_all, first_sub, sub_count)
    first_tile_own = lax.dynamic_slice_in_dim(first_tile_all, first_sub, sub_count)
    south_own = jnp.broadcast_to(south_one, (sub_count,))
    north_own = jnp.broadcast_to(north_one, (sub_count,))
    counts = jnp.stack([west_own, east_own, south_own, north_own], axis=-1)

    residual = dual_rhs[:, 0] * face_mask(counts, block_len)[:, None, :]
    west_residual = from_behind(residual[sub_count - 1, :, : 2 * block_len], "gx", 1)
    south_residual = from_behind(residual[..., 2 * block_len :], "gy", 1)

    tile_codes = job_code[:, 0]
    job_count = tile_codes.shape[0]
    is_valid = tile_codes >= 0
    owner_gx = jnp.where(is_valid, tile_codes // (NB * NB) // sub_count, 0)
    slot_cap = (sub_count * NB * (NB + 1) // 2 + gx_count - 1) // gx_count
    job_order = jnp.arange(job_count, dtype=jnp.int32)
    same_owner = (
        (owner_gx[:, None] == owner_gx[None, :])
        & is_valid[None, :]
        & (job_order[None, :] < job_order[:, None])
    )
    slot_rank = jnp.sum(same_owner.astype(jnp.int32), axis=1)
    send_slot = jnp.where(is_valid & (slot_rank < slot_cap), owner_gx * slot_cap + slot_rank, -1)
    slot_count = gx_count * slot_cap
    send_tiles = tiles_packed(send_slot, factor_panels, slot_count)
    send_tiles = send_tiles.reshape(gx_count, slot_cap * block_len, block_len)
    got_tiles = lax.all_to_all(send_tiles, "gx", split_axis=0, concat_axis=0, tiled=True)
    got_tiles = got_tiles.reshape(slot_count, block_len, block_len)

    source, alive = logical_slots(counts)
    row_slot = source[:, :, None]
    col_slot = source[:, None, :]
    low_slot = jnp.minimum(row_slot, col_slot)
    high_slot = jnp.maximum(row_slot, col_slot)
    nb = blocks_own[:, None, None]
    pair_index = low_slot * nb - low_slot * (low_slot - 1) // 2 + (high_slot - low_slot)
    tile_number = first_tile_own[:, None, None] + pair_index
    local_number = tile_number - first_tile_own[0]
    got_slot = tile_number % gx_count * slot_cap + local_number // gx_count
    both_alive = alive[:, :, None] & alive[:, None, :]
    matrix_mode = both_alive.astype(jnp.int32)
    matrix_from = jnp.where(both_alive, jnp.clip(got_slot, 0, slot_count - 1), 0)
    matrices = matrix_tiles(
        jnp.stack([matrix_from.reshape(-1), matrix_mode.reshape(-1)]), got_tiles, sub_count, NB
    )

    cases = residual.shape[1]
    cheb_center = (CHEB_HIGH + CHEB_LOW) / 2.0
    cheb_radius = (CHEB_HIGH - CHEB_LOW) / 2.0
    cheb_ratio = cheb_center / cheb_radius
    cheb_rho = 1.0 / cheb_ratio
    update = residual / cheb_center
    west_update = west_residual / cheb_center
    south_update = south_residual / cheb_center
    multipliers = jnp.zeros_like(residual)
    for sweep in range(ITERS):
        multipliers = multipliers + update
        east_part = update[..., : 2 * block_len]
        to_north_part = update[..., 2 * block_len :]
        west_in = -jnp.concatenate([west_update[None], east_part[: sub_count - 1]], axis=0)
        local_vec = jnp.concatenate([west_in, east_part, -south_update, to_north_part], axis=-1)
        high_f = lax.reduce_precision(local_vec, exponent_bits=8, mantissa_bits=7)
        high = high_f.astype(jnp.bfloat16)
        low = (local_vec - high_f).astype(jnp.bfloat16)
        both = jnp.einsum(
            "ncm,nmk->nck",
            jnp.concatenate([high, low], axis=1),
            matrices,
            preferred_element_type=jnp.float32,
        )
        image = both[:, :cases] + both[:, cases:]
        west_part = image[..., : 2 * block_len]
        split_east_part = image[..., 2 * block_len : 4 * block_len]
        south_part = image[..., 4 * block_len : 5 * block_len]
        split_north_part = image[..., 5 * block_len :]
        from_east = from_behind(west_part[0], "gx", -1)
        from_north = from_behind(south_part, "gy", -1)
        last = sweep == ITERS - 1
        if not last:
            west_east_part = from_behind(split_east_part[sub_count - 1], "gx", 1)
            south_north_part = from_behind(split_north_part, "gy", 1)
        east_near = jnp.concatenate([west_part[1:], from_east[None]], axis=0)
        residual = residual - jnp.concatenate(
            [split_east_part - east_near, split_north_part - from_north], axis=-1
        )
        rho_next = 1.0 / (2.0 * cheb_ratio - cheb_rho)
        keep = rho_next * cheb_rho
        step = 2.0 * rho_next / cheb_radius
        update = keep * update + step * residual
        if not last:
            west_residual = west_residual - (west_east_part - west_part[0])
            south_residual = south_residual - (south_north_part - south_part)
            west_update = keep * west_update + step * west_residual
            south_update = keep * south_update + step * south_residual
        cheb_rho = rho_next
    return (multipliers[:, None], residual[:, None])


def solution(mesh):
    in_specs = (
        P(None, "gy"),
        P("gx", "gy"),
        P("gx", "gy", None, None, None),
        P("gx", "gy", None, None),
    )
    out_specs = (P("gx", "gy", None, None), P("gx", "gy", None, None))
    return jax.shard_map(shards, mesh=mesh, in_specs=in_specs, out_specs=out_specs, check_vma=False)
```

```python
from functools import partial

import jax
import jax.numpy as jnp
from jax import lax
from jax.experimental import pallas as pl
from jax.experimental.pallas import tpu as pltpu
from jax.sharding import PartitionSpec as P

NB = 6
ITERS = 4


CHEB_LOW = 0.2
CHEB_HIGH = 7.0


def from_behind(value, axis, steps):
    count = lax.axis_size(axis)
    initial, last = (max(0, -steps), min(count, count - steps))
    return lax.ppermute(value, axis, [(source, source + steps) for source in range(initial, last)])


def _pack_kernel(table_ref, tiles_ref, out_ref, *, rows, block_len):
    for r in range(rows):
        tile = tiles_ref[table_ref[0, r]]
        keep = table_ref[1, r] != 0
        out_ref[r * block_len : (r + 1) * block_len, :] = jnp.where(keep, tile, jnp.zeros_like(tile))


def pack_tiles(table, tiles, rows):
    block_len = tiles.shape[-1]
    size = 2 * block_len * block_len
    return pl.pallas_call(
        partial(_pack_kernel, rows=rows, block_len=block_len),
        out_shape=jax.ShapeDtypeStruct((rows * block_len, block_len), tiles.dtype),
        in_specs=[
            pl.BlockSpec(memory_space=pltpu.SMEM),
            pl.BlockSpec(memory_space=pltpu.VMEM),
        ],
        out_specs=pl.BlockSpec(memory_space=pltpu.VMEM),
        cost_estimate=pl.CostEstimate(
            flops=0, transcendentals=0, bytes_accessed=(tiles.shape[0] + rows) * size
        ),
    )(table, tiles)


def _matrix_kernel(table_ref, tiles_ref, out_ref, *, subs, blocks, block_len):
    for s in range(subs):
        for p in range(blocks):
            for q in range(p, blocks):
                entry = (s * blocks + p) * blocks + q
                tile = tiles_ref[table_ref[0, entry]]
                keep = table_ref[1, entry] != 0
                tile = jnp.where(keep, tile, jnp.zeros_like(tile))
                out_ref[s, p * block_len : (p + 1) * block_len, q * block_len : (q + 1) * block_len] = tile
                if q > p:
                    out_ref[s, q * block_len : (q + 1) * block_len, p * block_len : (p + 1) * block_len] = (
                        tile.astype(jnp.float32).T.astype(tile.dtype)
                    )


def matrix_tiles(table, tiles, subs, blocks):
    block_len = tiles.shape[-1]
    size = 2 * block_len * block_len
    width = blocks * block_len
    return pl.pallas_call(
        partial(_matrix_kernel, subs=subs, blocks=blocks, block_len=block_len),
        out_shape=jax.ShapeDtypeStruct((subs, width, width), tiles.dtype),
        in_specs=[
            pl.BlockSpec(memory_space=pltpu.SMEM),
            pl.BlockSpec(memory_space=pltpu.VMEM),
        ],
        out_specs=pl.BlockSpec(memory_space=pltpu.VMEM),
        cost_estimate=pl.CostEstimate(
            flops=0, transcendentals=0, bytes_accessed=(tiles.shape[0] + subs * blocks * blocks) * size
        ),
    )(table, tiles)


def face_mask(counts, block_len):
    east_lane = jnp.arange(2 * block_len, dtype=jnp.int32) // block_len
    east_ok = east_lane < counts[..., 1:2]
    north_ok = jnp.zeros((block_len,), jnp.int32) < counts[..., 3:4]
    return jnp.concatenate([east_ok, north_ok], axis=-1).astype(jnp.float32)


def logical_slots(counts):
    west_n = counts[:, 0:1]
    east_n = counts[:, 1:2]
    south_n = counts[:, 2:3]
    north_n = counts[:, 3:4]
    within = jnp.array([0, 1, 0, 1, 0, 0], jnp.int32)[None, :]
    zero = jnp.zeros_like(west_n)
    offsets = jnp.concatenate(
        [zero, zero, west_n, west_n, west_n + east_n, west_n + east_n + south_n], axis=1
    )
    limits = jnp.concatenate([west_n, west_n, east_n, east_n, south_n, north_n], axis=1)
    return offsets + within, within < limits


def shards(east_blocks, job_code, factor_panels, dual_rhs):
    gx_count = lax.axis_size("gx")
    gy_count = lax.axis_size("gy")
    gx_index = lax.axis_index("gx")
    gy_index = lax.axis_index("gy")
    block_len = factor_panels.shape[-1]
    sub_count = dual_rhs.shape[0]
    column = east_blocks[:, 0]
    west_column = jnp.concatenate([jnp.zeros((1,), jnp.int32), column[:-1]])
    south_one = (gy_index > 0).astype(jnp.int32)
    north_one = (gy_index < gy_count - 1).astype(jnp.int32)
    blocks_all = west_column + column + south_one + north_one
    tiles_all = blocks_all * (blocks_all + 1) // 2
    first_tile_all = jnp.cumsum(tiles_all) - tiles_all
    first_sub = gx_index * sub_count
    east_own = lax.dynamic_slice_in_dim(column, first_sub, sub_count)
    west_own = lax.dynamic_slice_in_dim(west_column, first_sub, sub_count)
    blocks_own = lax.dynamic_slice_in_dim(blocks_all, first_sub, sub_count)
    first_tile_own = lax.dynamic_slice_in_dim(first_tile_all, first_sub, sub_count)
    south_own = jnp.broadcast_to(south_one, (sub_count,))
    north_own = jnp.broadcast_to(north_one, (sub_count,))
    counts = jnp.stack([west_own, east_own, south_own, north_own], axis=-1)

    residual = dual_rhs[:, 0] * face_mask(counts, block_len)[:, None, :]
    west_residual = from_behind(residual[sub_count - 1, :, : 2 * block_len], "gx", 1)
    south_residual = from_behind(residual[..., 2 * block_len :], "gy", 1)

    tiles = jnp.einsum(
        "jka,jkb->jab",
        factor_panels[:, 0, 0],
        factor_panels[:, 0, 1],
        preferred_element_type=jnp.float32,
    ).astype(jnp.bfloat16)
    tile_codes = job_code[:, 0]
    job_count = tile_codes.shape[0]
    is_valid = tile_codes >= 0
    owner_gx = jnp.where(is_valid, tile_codes // (NB * NB) // sub_count, 0)
    slot_cap = (sub_count * NB * (NB + 1) // 2 + gx_count - 1) // gx_count
    job_order = jnp.arange(job_count, dtype=jnp.int32)
    same_owner = (
        (owner_gx[:, None] == owner_gx[None, :])
        & is_valid[None, :]
        & (job_order[None, :] < job_order[:, None])
    )
    slot_rank = jnp.sum(same_owner.astype(jnp.int32), axis=1)
    send_slot = jnp.where(is_valid & (slot_rank < slot_cap), owner_gx * slot_cap + slot_rank, -1)
    slot_count = gx_count * slot_cap
    send_hit = send_slot[None, :] == jnp.arange(slot_count, dtype=jnp.int32)[:, None]
    send_from = jnp.sum(jnp.where(send_hit, job_order[None, :], 0), axis=1)
    send_mode = jnp.any(send_hit, axis=1).astype(jnp.int32)
    send_tiles = pack_tiles(jnp.stack([send_from, send_mode]), tiles, slot_count)
    send_tiles = send_tiles.reshape(gx_count, slot_cap * block_len, block_len)
    got_tiles = lax.all_to_all(send_tiles, "gx", split_axis=0, concat_axis=0, tiled=True)
    got_tiles = got_tiles.reshape(slot_count, block_len, block_len)

    source, alive = logical_slots(counts)
    row_slot = source[:, :, None]
    col_slot = source[:, None, :]
    low_slot = jnp.minimum(row_slot, col_slot)
    high_slot = jnp.maximum(row_slot, col_slot)
    nb = blocks_own[:, None, None]
    pair_index = low_slot * nb - low_slot * (low_slot - 1) // 2 + (high_slot - low_slot)
    tile_number = first_tile_own[:, None, None] + pair_index
    local_number = tile_number - first_tile_own[0]
    got_slot = tile_number % gx_count * slot_cap + local_number // gx_count
    both_alive = alive[:, :, None] & alive[:, None, :]
    matrix_mode = both_alive.astype(jnp.int32)
    matrix_from = jnp.where(both_alive, jnp.clip(got_slot, 0, slot_count - 1), 0)
    matrices = matrix_tiles(
        jnp.stack([matrix_from.reshape(-1), matrix_mode.reshape(-1)]), got_tiles, sub_count, NB
    )

    cases = residual.shape[1]
    cheb_center = (CHEB_HIGH + CHEB_LOW) / 2.0
    cheb_radius = (CHEB_HIGH - CHEB_LOW) / 2.0
    cheb_ratio = cheb_center / cheb_radius
    cheb_rho = 1.0 / cheb_ratio
    update = residual / cheb_center
    west_update = west_residual / cheb_center
    south_update = south_residual / cheb_center
    multipliers = jnp.zeros_like(residual)
    for sweep in range(ITERS):
        multipliers = multipliers + update
        east_part = update[..., : 2 * block_len]
        to_north_part = update[..., 2 * block_len :]
        west_in = -jnp.concatenate([west_update[None], east_part[: sub_count - 1]], axis=0)
        local_vec = jnp.concatenate([west_in, east_part, -south_update, to_north_part], axis=-1)
        high_f = lax.reduce_precision(local_vec, exponent_bits=8, mantissa_bits=7)
        high = high_f.astype(jnp.bfloat16)
        low = (local_vec - high_f).astype(jnp.bfloat16)
        both = jnp.einsum(
            "ncm,nmk->nck",
            jnp.concatenate([high, low], axis=1),
            matrices,
            preferred_element_type=jnp.float32,
        )
        image = both[:, :cases] + both[:, cases:]
        west_part = image[..., : 2 * block_len]
        split_east_part = image[..., 2 * block_len : 4 * block_len]
        south_part = image[..., 4 * block_len : 5 * block_len]
        split_north_part = image[..., 5 * block_len :]
        from_east = from_behind(west_part[0], "gx", -1)
        from_north = from_behind(south_part, "gy", -1)
        last = sweep == ITERS - 1
        if not last:
            west_east_part = from_behind(split_east_part[sub_count - 1], "gx", 1)
            south_north_part = from_behind(split_north_part, "gy", 1)
        east_near = jnp.concatenate([west_part[1:], from_east[None]], axis=0)
        residual = residual - jnp.concatenate(
            [split_east_part - east_near, split_north_part - from_north], axis=-1
        )
        rho_next = 1.0 / (2.0 * cheb_ratio - cheb_rho)
        keep = rho_next * cheb_rho
        step = 2.0 * rho_next / cheb_radius
        update = keep * update + step * residual
        if not last:
            west_residual = west_residual - (west_east_part - west_part[0])
            south_residual = south_residual - (south_north_part - south_part)
            west_update = keep * west_update + step * west_residual
            south_update = keep * south_update + step * south_residual
        cheb_rho = rho_next
    return (multipliers[:, None], residual[:, None])


def solution(mesh):
    in_specs = (
        P(None, "gy"),
        P("gx", "gy"),
        P("gx", "gy", None, None, None),
        P("gx", "gy", None, None),
    )
    out_specs = (P("gx", "gy", None, None), P("gx", "gy", None, None))
    return jax.shard_map(shards, mesh=mesh, in_specs=in_specs, out_specs=out_specs, check_vma=False)
```

```python
from functools import partial

import jax
import jax.numpy as jnp
from jax import lax
from jax.experimental import pallas as pl
from jax.experimental.pallas import tpu as pltpu
from jax.sharding import PartitionSpec as P

NB = 6
ITERS = 4


CHEB_LOW = 0.2
CHEB_HIGH = 7.0


def from_behind(value, axis, steps):
    count = lax.axis_size(axis)
    initial, last = (max(0, -steps), min(count, count - steps))
    return lax.ppermute(value, axis, [(source, source + steps) for source in range(initial, last)])


def _pack_kernel(table_ref, tiles_ref, out_ref, *, rows, block_len):
    for r in range(rows):
        tile = tiles_ref[table_ref[0, r]]
        keep = table_ref[1, r] != 0
        out_ref[r * block_len : (r + 1) * block_len, :] = jnp.where(keep, tile, jnp.zeros_like(tile))


def pack_tiles(table, tiles, rows):
    block_len = tiles.shape[-1]
    size = 2 * block_len * block_len
    return pl.pallas_call(
        partial(_pack_kernel, rows=rows, block_len=block_len),
        out_shape=jax.ShapeDtypeStruct((rows * block_len, block_len), tiles.dtype),
        in_specs=[
            pl.BlockSpec(memory_space=pltpu.SMEM),
            pl.BlockSpec(memory_space=pltpu.VMEM),
        ],
        out_specs=pl.BlockSpec(memory_space=pltpu.VMEM),
        cost_estimate=pl.CostEstimate(
            flops=0, transcendentals=0, bytes_accessed=(tiles.shape[0] + rows) * size
        ),
    )(table, tiles)


def _matrix_kernel(table_ref, tiles_ref, out_ref, *, subs, blocks, block_len):
    for s in range(subs):
        for p in range(blocks):
            for q in range(p, blocks):
                entry = (s * blocks + p) * blocks + q
                tile = tiles_ref[table_ref[0, entry]]
                keep = table_ref[1, entry] != 0
                tile = jnp.where(keep, tile, jnp.zeros_like(tile))
                out_ref[s, p * block_len : (p + 1) * block_len, q * block_len : (q + 1) * block_len] = tile
                if q > p:
                    out_ref[s, q * block_len : (q + 1) * block_len, p * block_len : (p + 1) * block_len] = (
                        tile.astype(jnp.float32).T.astype(tile.dtype)
                    )


def matrix_tiles(table, tiles, subs, blocks):
    block_len = tiles.shape[-1]
    size = 2 * block_len * block_len
    width = blocks * block_len
    return pl.pallas_call(
        partial(_matrix_kernel, subs=subs, blocks=blocks, block_len=block_len),
        out_shape=jax.ShapeDtypeStruct((subs, width, width), tiles.dtype),
        in_specs=[
            pl.BlockSpec(memory_space=pltpu.SMEM),
            pl.BlockSpec(memory_space=pltpu.VMEM),
        ],
        out_specs=pl.BlockSpec(memory_space=pltpu.VMEM),
        cost_estimate=pl.CostEstimate(
            flops=0, transcendentals=0, bytes_accessed=(tiles.shape[0] + subs * blocks * blocks) * size
        ),
    )(table, tiles)


def face_mask(counts, block_len):
    east_lane = jnp.arange(2 * block_len, dtype=jnp.int32) // block_len
    east_ok = east_lane < counts[..., 1:2]
    north_ok = jnp.zeros((block_len,), jnp.int32) < counts[..., 3:4]
    return jnp.concatenate([east_ok, north_ok], axis=-1).astype(jnp.float32)


def logical_slots(counts):
    west_n = counts[:, 0:1]
    east_n = counts[:, 1:2]
    south_n = counts[:, 2:3]
    north_n = counts[:, 3:4]
    within = jnp.array([0, 1, 0, 1, 0, 0], jnp.int32)[None, :]
    zero = jnp.zeros_like(west_n)
    offsets = jnp.concatenate(
        [zero, zero, west_n, west_n, west_n + east_n, west_n + east_n + south_n], axis=1
    )
    limits = jnp.concatenate([west_n, west_n, east_n, east_n, south_n, north_n], axis=1)
    return offsets + within, within < limits


def shards(east_blocks, job_code, factor_panels, dual_rhs):
    gx_count = lax.axis_size("gx")
    gy_count = lax.axis_size("gy")
    gx_index = lax.axis_index("gx")
    gy_index = lax.axis_index("gy")
    block_len = factor_panels.shape[-1]
    sub_count = dual_rhs.shape[0]
    column = east_blocks[:, 0]
    west_column = jnp.concatenate([jnp.zeros((1,), jnp.int32), column[:-1]])
    south_one = (gy_index > 0).astype(jnp.int32)
    north_one = (gy_index < gy_count - 1).astype(jnp.int32)
    blocks_all = west_column + column + south_one + north_one
    tiles_all = blocks_all * (blocks_all + 1) // 2
    first_tile_all = jnp.cumsum(tiles_all) - tiles_all
    first_sub = gx_index * sub_count
    east_own = lax.dynamic_slice_in_dim(column, first_sub, sub_count)
    west_own = lax.dynamic_slice_in_dim(west_column, first_sub, sub_count)
    blocks_own = lax.dynamic_slice_in_dim(blocks_all, first_sub, sub_count)
    first_tile_own = lax.dynamic_slice_in_dim(first_tile_all, first_sub, sub_count)
    south_own = jnp.broadcast_to(south_one, (sub_count,))
    north_own = jnp.broadcast_to(north_one, (sub_count,))
    counts = jnp.stack([west_own, east_own, south_own, north_own], axis=-1)

    residual = dual_rhs[:, 0] * face_mask(counts, block_len)[:, None, :]
    west_residual = from_behind(residual[sub_count - 1, :, : 2 * block_len], "gx", 1)
    south_residual = from_behind(residual[..., 2 * block_len :], "gy", 1)

    tiles = jnp.einsum(
        "jka,jkb->jab",
        factor_panels[:, 0, 0],
        factor_panels[:, 0, 1],
        preferred_element_type=jnp.float32,
    ).astype(jnp.bfloat16)
    tile_codes = job_code[:, 0]
    job_count = tile_codes.shape[0]
    is_valid = tile_codes >= 0
    owner_gx = jnp.where(is_valid, tile_codes // (NB * NB) // sub_count, 0)
    slot_cap = (sub_count * NB * (NB + 1) // 2 + gx_count - 1) // gx_count
    job_order = jnp.arange(job_count, dtype=jnp.int32)
    same_owner = (
        (owner_gx[:, None] == owner_gx[None, :])
        & is_valid[None, :]
        & (job_order[None, :] < job_order[:, None])
    )
    slot_rank = jnp.sum(same_owner.astype(jnp.int32), axis=1)
    send_slot = jnp.where(is_valid & (slot_rank < slot_cap), owner_gx * slot_cap + slot_rank, -1)
    slot_count = gx_count * slot_cap
    send_hit = send_slot[None, :] == jnp.arange(slot_count, dtype=jnp.int32)[:, None]
    send_from = jnp.sum(jnp.where(send_hit, job_order[None, :], 0), axis=1)
    send_mode = jnp.any(send_hit, axis=1).astype(jnp.int32)
    send_tiles = pack_tiles(jnp.stack([send_from, send_mode]), tiles, slot_count)
    send_tiles = send_tiles.reshape(gx_count, slot_cap * block_len, block_len)
    got_tiles = lax.all_to_all(send_tiles, "gx", split_axis=0, concat_axis=0, tiled=True)
    got_tiles = got_tiles.reshape(slot_count, block_len, block_len)

    source, alive = logical_slots(counts)
    row_slot = source[:, :, None]
    col_slot = source[:, None, :]
    low_slot = jnp.minimum(row_slot, col_slot)
    high_slot = jnp.maximum(row_slot, col_slot)
    nb = blocks_own[:, None, None]
    pair_index = low_slot * nb - low_slot * (low_slot - 1) // 2 + (high_slot - low_slot)
    tile_number = first_tile_own[:, None, None] + pair_index
    local_number = tile_number - first_tile_own[0]
    got_slot = tile_number % gx_count * slot_cap + local_number // gx_count
    both_alive = alive[:, :, None] & alive[:, None, :]
    matrix_mode = both_alive.astype(jnp.int32)
    matrix_from = jnp.where(both_alive, jnp.clip(got_slot, 0, slot_count - 1), 0)
    matrices = matrix_tiles(
        jnp.stack([matrix_from.reshape(-1), matrix_mode.reshape(-1)]), got_tiles, sub_count, NB
    )

    cases = residual.shape[1]
    cheb_center = (CHEB_HIGH + CHEB_LOW) / 2.0
    cheb_radius = (CHEB_HIGH - CHEB_LOW) / 2.0
    cheb_ratio = cheb_center / cheb_radius
    cheb_rho = 1.0 / cheb_ratio
    update = residual / cheb_center
    west_update = west_residual / cheb_center
    south_update = south_residual / cheb_center
    multipliers = jnp.zeros_like(residual)
    for sweep in range(ITERS):
        multipliers = multipliers + update
        east_part = update[..., : 2 * block_len]
        to_north_part = update[..., 2 * block_len :]
        west_in = -jnp.concatenate([west_update[None], east_part[: sub_count - 1]], axis=0)
        local_vec = jnp.concatenate([west_in, east_part, -south_update, to_north_part], axis=-1)
        high_f = lax.reduce_precision(local_vec, exponent_bits=8, mantissa_bits=7)
        high = high_f.astype(jnp.bfloat16)
        low = (local_vec - high_f).astype(jnp.bfloat16)
        both = jnp.einsum(
            "ncm,nmk->nck",
            jnp.concatenate([high, low], axis=1),
            matrices,
            preferred_element_type=jnp.float32,
        )
        image = both[:, :cases] + both[:, cases:]
        west_part = image[..., : 2 * block_len]
        split_east_part = image[..., 2 * block_len : 4 * block_len]
        south_part = image[..., 4 * block_len : 5 * block_len]
        split_north_part = image[..., 5 * block_len :]
        from_east = from_behind(west_part[0], "gx", -1)
        from_north = from_behind(south_part.astype(jnp.bfloat16), "gy", -1).astype(jnp.float32)
        last = sweep == ITERS - 1
        if not last:
            west_east_part = from_behind(split_east_part[sub_count - 1], "gx", 1)
            south_north_part = from_behind(split_north_part.astype(jnp.bfloat16), "gy", 1).astype(jnp.float32)
        east_near = jnp.concatenate([west_part[1:], from_east[None]], axis=0)
        residual = residual - jnp.concatenate(
            [split_east_part - east_near, split_north_part - from_north], axis=-1
        )
        rho_next = 1.0 / (2.0 * cheb_ratio - cheb_rho)
        keep = rho_next * cheb_rho
        step = 2.0 * rho_next / cheb_radius
        update = keep * update + step * residual
        if not last:
            west_residual = west_residual - (west_east_part - west_part[0])
            south_residual = south_residual - (south_north_part - south_part)
            west_update = keep * west_update + step * west_residual
            south_update = keep * south_update + step * south_residual
        cheb_rho = rho_next
    return (multipliers[:, None], residual[:, None])


def solution(mesh):
    in_specs = (
        P(None, "gy"),
        P("gx", "gy"),
        P("gx", "gy", None, None, None),
        P("gx", "gy", None, None),
    )
    out_specs = (P("gx", "gy", None, None), P("gx", "gy", None, None))
    return jax.shard_map(shards, mesh=mesh, in_specs=in_specs, out_specs=out_specs, check_vma=False)
```

```python
from functools import partial

import jax
import jax.numpy as jnp
from jax import lax
from jax.experimental import pallas as pl
from jax.experimental.pallas import tpu as pltpu
from jax.sharding import PartitionSpec as P

NB = 6
ITERS = 4


CHEB_LOW = 0.2
CHEB_HIGH = 7.0


def from_behind(value, axis, steps):
    count = lax.axis_size(axis)
    initial, last = (max(0, -steps), min(count, count - steps))
    return lax.ppermute(value, axis, [(source, source + steps) for source in range(initial, last)])


def _pack_kernel(code_ref, tiles_ref, out_ref, *, per_owner, owner_subs, block_len):
    out_ref[...] = jnp.zeros_like(out_ref)
    previous = jnp.int32(-1)
    rank = jnp.int32(0)
    for j in range(tiles_ref.shape[0]):
        code = code_ref[j]
        owner = lax.div(jnp.maximum(code, 0), jnp.int32(NB * NB * owner_subs))
        rank = jnp.where(owner == previous, rank + 1, 0)
        previous = owner
        slot = owner * per_owner + rank

        @pl.when((code >= 0) & (rank < per_owner))
        def _():
            out_ref[pl.ds(pl.multiple_of(slot * block_len, block_len), block_len), :] = tiles_ref[j]


def pack_tiles(codes, tiles, owners, per_owner, owner_subs):
    block_len = tiles.shape[-1]
    rows = owners * per_owner
    size = 2 * block_len * block_len
    return pl.pallas_call(
        partial(_pack_kernel, per_owner=per_owner, owner_subs=owner_subs, block_len=block_len),
        out_shape=jax.ShapeDtypeStruct((rows * block_len, block_len), tiles.dtype),
        in_specs=[
            pl.BlockSpec(memory_space=pltpu.SMEM),
            pl.BlockSpec(memory_space=pltpu.VMEM),
        ],
        out_specs=pl.BlockSpec(memory_space=pltpu.VMEM),
        cost_estimate=pl.CostEstimate(
            flops=0, transcendentals=0, bytes_accessed=(tiles.shape[0] + rows) * size
        ),
    )(codes, tiles)


def _matrix_kernel(table_ref, tiles_ref, out_ref, *, subs, blocks, block_len):
    for s in range(subs):
        for p in range(blocks):
            for q in range(p, blocks):
                entry = (s * blocks + p) * blocks + q
                tile = tiles_ref[table_ref[0, entry]]
                keep = table_ref[1, entry] != 0
                tile = jnp.where(keep, tile, jnp.zeros_like(tile))
                out_ref[s, p * block_len : (p + 1) * block_len, q * block_len : (q + 1) * block_len] = tile
                if q > p:
                    out_ref[s, q * block_len : (q + 1) * block_len, p * block_len : (p + 1) * block_len] = (
                        tile.astype(jnp.float32).T.astype(tile.dtype)
                    )


def matrix_tiles(table, tiles, subs, blocks):
    block_len = tiles.shape[-1]
    size = 2 * block_len * block_len
    width = blocks * block_len
    return pl.pallas_call(
        partial(_matrix_kernel, subs=subs, blocks=blocks, block_len=block_len),
        out_shape=jax.ShapeDtypeStruct((subs, width, width), tiles.dtype),
        in_specs=[
            pl.BlockSpec(memory_space=pltpu.SMEM),
            pl.BlockSpec(memory_space=pltpu.VMEM),
        ],
        out_specs=pl.BlockSpec(memory_space=pltpu.VMEM),
        cost_estimate=pl.CostEstimate(
            flops=0, transcendentals=0, bytes_accessed=(tiles.shape[0] + subs * blocks * blocks) * size
        ),
    )(table, tiles)


def face_mask(counts, block_len):
    east_lane = jnp.arange(2 * block_len, dtype=jnp.int32) // block_len
    east_ok = east_lane < counts[..., 1:2]
    north_ok = jnp.zeros((block_len,), jnp.int32) < counts[..., 3:4]
    return jnp.concatenate([east_ok, north_ok], axis=-1).astype(jnp.float32)


def logical_slots(counts):
    west_n = counts[:, 0:1]
    east_n = counts[:, 1:2]
    south_n = counts[:, 2:3]
    north_n = counts[:, 3:4]
    within = jnp.array([0, 1, 0, 1, 0, 0], jnp.int32)[None, :]
    zero = jnp.zeros_like(west_n)
    offsets = jnp.concatenate(
        [zero, zero, west_n, west_n, west_n + east_n, west_n + east_n + south_n], axis=1
    )
    limits = jnp.concatenate([west_n, west_n, east_n, east_n, south_n, north_n], axis=1)
    return offsets + within, within < limits


def shards(east_blocks, job_code, factor_panels, dual_rhs):
    gx_count = lax.axis_size("gx")
    gy_count = lax.axis_size("gy")
    gx_index = lax.axis_index("gx")
    gy_index = lax.axis_index("gy")
    block_len = factor_panels.shape[-1]
    sub_count = dual_rhs.shape[0]
    column = east_blocks[:, 0]
    west_column = jnp.concatenate([jnp.zeros((1,), jnp.int32), column[:-1]])
    south_one = (gy_index > 0).astype(jnp.int32)
    north_one = (gy_index < gy_count - 1).astype(jnp.int32)
    blocks_all = west_column + column + south_one + north_one
    tiles_all = blocks_all * (blocks_all + 1) // 2
    first_tile_all = jnp.cumsum(tiles_all) - tiles_all
    first_sub = gx_index * sub_count
    east_own = lax.dynamic_slice_in_dim(column, first_sub, sub_count)
    west_own = lax.dynamic_slice_in_dim(west_column, first_sub, sub_count)
    blocks_own = lax.dynamic_slice_in_dim(blocks_all, first_sub, sub_count)
    first_tile_own = lax.dynamic_slice_in_dim(first_tile_all, first_sub, sub_count)
    south_own = jnp.broadcast_to(south_one, (sub_count,))
    north_own = jnp.broadcast_to(north_one, (sub_count,))
    counts = jnp.stack([west_own, east_own, south_own, north_own], axis=-1)

    residual = dual_rhs[:, 0] * face_mask(counts, block_len)[:, None, :]
    west_residual = from_behind(residual[sub_count - 1, :, : 2 * block_len], "gx", 1)
    south_residual = from_behind(residual[..., 2 * block_len :], "gy", 1)

    tiles = jnp.einsum(
        "jka,jkb->jab",
        factor_panels[:, 0, 0],
        factor_panels[:, 0, 1],
        preferred_element_type=jnp.float32,
    ).astype(jnp.bfloat16)
    slot_cap = (sub_count * NB * (NB + 1) // 2 + gx_count - 1) // gx_count
    slot_count = gx_count * slot_cap
    send_tiles = pack_tiles(job_code[:, 0], tiles, gx_count, slot_cap, sub_count)
    send_tiles = send_tiles.reshape(gx_count, slot_cap * block_len, block_len)
    got_tiles = lax.all_to_all(send_tiles, "gx", split_axis=0, concat_axis=0, tiled=True)
    got_tiles = got_tiles.reshape(slot_count, block_len, block_len)

    source, alive = logical_slots(counts)
    row_slot = source[:, :, None]
    col_slot = source[:, None, :]
    low_slot = jnp.minimum(row_slot, col_slot)
    high_slot = jnp.maximum(row_slot, col_slot)
    nb = blocks_own[:, None, None]
    pair_index = low_slot * nb - low_slot * (low_slot - 1) // 2 + (high_slot - low_slot)
    tile_number = first_tile_own[:, None, None] + pair_index
    local_number = tile_number - first_tile_own[0]
    got_slot = tile_number % gx_count * slot_cap + local_number // gx_count
    both_alive = alive[:, :, None] & alive[:, None, :]
    matrix_mode = both_alive.astype(jnp.int32)
    matrix_from = jnp.where(both_alive, jnp.clip(got_slot, 0, slot_count - 1), 0)
    matrices = matrix_tiles(
        jnp.stack([matrix_from.reshape(-1), matrix_mode.reshape(-1)]), got_tiles, sub_count, NB
    )

    cases = residual.shape[1]
    cheb_center = (CHEB_HIGH + CHEB_LOW) / 2.0
    cheb_radius = (CHEB_HIGH - CHEB_LOW) / 2.0
    cheb_ratio = cheb_center / cheb_radius
    cheb_rho = 1.0 / cheb_ratio
    update = residual / cheb_center
    west_update = west_residual / cheb_center
    south_update = south_residual / cheb_center
    multipliers = jnp.zeros_like(residual)
    for sweep in range(ITERS):
        multipliers = multipliers + update
        east_part = update[..., : 2 * block_len]
        to_north_part = update[..., 2 * block_len :]
        west_in = -jnp.concatenate([west_update[None], east_part[: sub_count - 1]], axis=0)
        local_vec = jnp.concatenate([west_in, east_part, -south_update, to_north_part], axis=-1)
        high_f = lax.reduce_precision(local_vec, exponent_bits=8, mantissa_bits=7)
        high = high_f.astype(jnp.bfloat16)
        low = (local_vec - high_f).astype(jnp.bfloat16)
        both = jnp.einsum(
            "ncm,nmk->nck",
            jnp.concatenate([high, low], axis=1),
            matrices,
            preferred_element_type=jnp.float32,
        )
        image = both[:, :cases] + both[:, cases:]
        west_part = image[..., : 2 * block_len]
        split_east_part = image[..., 2 * block_len : 4 * block_len]
        south_part = image[..., 4 * block_len : 5 * block_len]
        split_north_part = image[..., 5 * block_len :]
        from_east = from_behind(west_part[0], "gx", -1)
        from_north = from_behind(south_part, "gy", -1)
        last = sweep == ITERS - 1
        if not last:
            west_east_part = from_behind(split_east_part[sub_count - 1], "gx", 1)
            south_north_part = from_behind(split_north_part, "gy", 1)
        east_near = jnp.concatenate([west_part[1:], from_east[None]], axis=0)
        residual = residual - jnp.concatenate(
            [split_east_part - east_near, split_north_part - from_north], axis=-1
        )
        rho_next = 1.0 / (2.0 * cheb_ratio - cheb_rho)
        keep = rho_next * cheb_rho
        step = 2.0 * rho_next / cheb_radius
        update = keep * update + step * residual
        if not last:
            west_residual = west_residual - (west_east_part - west_part[0])
            south_residual = south_residual - (south_north_part - south_part)
            west_update = keep * west_update + step * west_residual
            south_update = keep * south_update + step * south_residual
        cheb_rho = rho_next
    return (multipliers[:, None], residual[:, None])


def solution(mesh):
    in_specs = (
        P(None, "gy"),
        P("gx", "gy"),
        P("gx", "gy", None, None, None),
        P("gx", "gy", None, None),
    )
    out_specs = (P("gx", "gy", None, None), P("gx", "gy", None, None))
    return jax.shard_map(shards, mesh=mesh, in_specs=in_specs, out_specs=out_specs, check_vma=False)
```

```python
from functools import partial

import jax
import jax.numpy as jnp
from jax import lax
from jax.experimental import pallas as pl
from jax.experimental.pallas import tpu as pltpu
from jax.sharding import PartitionSpec as P

NB = 6
ITERS = 4


CHEB_LOW = 0.2
CHEB_HIGH = 7.0


def from_behind(value, axis, steps):
    count = lax.axis_size(axis)
    initial, last = (max(0, -steps), min(count, count - steps))
    return lax.ppermute(value, axis, [(source, source + steps) for source in range(initial, last)])


def _pack_kernel(code_ref, tiles_ref, out_ref, *, per_owner, owner_subs, block_len):
    previous = jnp.int32(-1)
    rank = jnp.int32(0)
    for j in range(tiles_ref.shape[0]):
        code = code_ref[j]
        owner = lax.div(jnp.maximum(code, 0), jnp.int32(NB * NB * owner_subs))
        rank = jnp.where(owner == previous, rank + 1, 0)
        previous = owner
        slot = owner * per_owner + rank

        @pl.when((code >= 0) & (rank < per_owner))
        def _():
            out_ref[pl.ds(pl.multiple_of(slot * block_len, block_len), block_len), :] = tiles_ref[j]


def pack_tiles(codes, tiles, owners, per_owner, owner_subs):
    block_len = tiles.shape[-1]
    rows = owners * per_owner
    size = 2 * block_len * block_len
    return pl.pallas_call(
        partial(_pack_kernel, per_owner=per_owner, owner_subs=owner_subs, block_len=block_len),
        out_shape=jax.ShapeDtypeStruct((rows * block_len, block_len), tiles.dtype),
        in_specs=[
            pl.BlockSpec(memory_space=pltpu.SMEM),
            pl.BlockSpec(memory_space=pltpu.VMEM),
        ],
        out_specs=pl.BlockSpec(memory_space=pltpu.VMEM),
        cost_estimate=pl.CostEstimate(
            flops=0, transcendentals=0, bytes_accessed=(tiles.shape[0] + rows) * size
        ),
    )(codes, tiles)


def _matrix_kernel(table_ref, tiles_ref, out_ref, *, subs, blocks, block_len):
    for s in range(subs):
        for p in range(blocks):
            for q in range(p, blocks):
                entry = (s * blocks + p) * blocks + q
                tile = tiles_ref[table_ref[0, entry]]
                keep = table_ref[1, entry] != 0
                tile = jnp.where(keep, tile, jnp.zeros_like(tile))
                out_ref[s, p * block_len : (p + 1) * block_len, q * block_len : (q + 1) * block_len] = tile
                if q > p:
                    out_ref[s, q * block_len : (q + 1) * block_len, p * block_len : (p + 1) * block_len] = (
                        tile.T
                    )


def matrix_tiles(table, tiles, subs, blocks):
    block_len = tiles.shape[-1]
    size = 2 * block_len * block_len
    width = blocks * block_len
    return pl.pallas_call(
        partial(_matrix_kernel, subs=subs, blocks=blocks, block_len=block_len),
        out_shape=jax.ShapeDtypeStruct((subs, width, width), tiles.dtype),
        in_specs=[
            pl.BlockSpec(memory_space=pltpu.SMEM),
            pl.BlockSpec(memory_space=pltpu.VMEM),
        ],
        out_specs=pl.BlockSpec(memory_space=pltpu.VMEM),
        cost_estimate=pl.CostEstimate(
            flops=0, transcendentals=0, bytes_accessed=(tiles.shape[0] + subs * blocks * blocks) * size
        ),
    )(table, tiles)


def face_mask(counts, block_len):
    east_lane = jnp.arange(2 * block_len, dtype=jnp.int32) // block_len
    east_ok = east_lane < counts[..., 1:2]
    north_ok = jnp.zeros((block_len,), jnp.int32) < counts[..., 3:4]
    return jnp.concatenate([east_ok, north_ok], axis=-1).astype(jnp.float32)


def logical_slots(counts):
    west_n = counts[:, 0:1]
    east_n = counts[:, 1:2]
    south_n = counts[:, 2:3]
    north_n = counts[:, 3:4]
    within = jnp.array([0, 1, 0, 1, 0, 0], jnp.int32)[None, :]
    zero = jnp.zeros_like(west_n)
    offsets = jnp.concatenate(
        [zero, zero, west_n, west_n, west_n + east_n, west_n + east_n + south_n], axis=1
    )
    limits = jnp.concatenate([west_n, west_n, east_n, east_n, south_n, north_n], axis=1)
    return offsets + within, within < limits


def shards(east_blocks, job_code, factor_panels, dual_rhs):
    gx_count = lax.axis_size("gx")
    gy_count = lax.axis_size("gy")
    gx_index = lax.axis_index("gx")
    gy_index = lax.axis_index("gy")
    block_len = factor_panels.shape[-1]
    sub_count = dual_rhs.shape[0]
    column = east_blocks[:, 0]
    west_column = jnp.concatenate([jnp.zeros((1,), jnp.int32), column[:-1]])
    south_one = (gy_index > 0).astype(jnp.int32)
    north_one = (gy_index < gy_count - 1).astype(jnp.int32)
    blocks_all = west_column + column + south_one + north_one
    tiles_all = blocks_all * (blocks_all + 1) // 2
    first_tile_all = jnp.cumsum(tiles_all) - tiles_all
    first_sub = gx_index * sub_count
    east_own = lax.dynamic_slice_in_dim(column, first_sub, sub_count)
    west_own = lax.dynamic_slice_in_dim(west_column, first_sub, sub_count)
    blocks_own = lax.dynamic_slice_in_dim(blocks_all, first_sub, sub_count)
    first_tile_own = lax.dynamic_slice_in_dim(first_tile_all, first_sub, sub_count)
    south_own = jnp.broadcast_to(south_one, (sub_count,))
    north_own = jnp.broadcast_to(north_one, (sub_count,))
    counts = jnp.stack([west_own, east_own, south_own, north_own], axis=-1)

    residual = dual_rhs[:, 0] * face_mask(counts, block_len)[:, None, :]
    west_residual = from_behind(residual[sub_count - 1, :, : 2 * block_len], "gx", 1)
    south_residual = from_behind(residual[..., 2 * block_len :], "gy", 1)

    tiles = jnp.einsum(
        "jka,jkb->jab",
        factor_panels[:, 0, 0],
        factor_panels[:, 0, 1],
        preferred_element_type=jnp.float32,
    ).astype(jnp.bfloat16)
    slot_cap = (sub_count * NB * (NB + 1) // 2 + gx_count - 1) // gx_count
    slot_count = gx_count * slot_cap
    send_tiles = pack_tiles(job_code[:, 0], tiles, gx_count, slot_cap, sub_count)
    send_tiles = send_tiles.reshape(gx_count, slot_cap * block_len, block_len)
    got_tiles = lax.all_to_all(send_tiles, "gx", split_axis=0, concat_axis=0, tiled=True)
    got_tiles = got_tiles.reshape(slot_count, block_len, block_len)

    source, alive = logical_slots(counts)
    row_slot = source[:, :, None]
    col_slot = source[:, None, :]
    low_slot = jnp.minimum(row_slot, col_slot)
    high_slot = jnp.maximum(row_slot, col_slot)
    nb = blocks_own[:, None, None]
    pair_index = low_slot * nb - low_slot * (low_slot - 1) // 2 + (high_slot - low_slot)
    tile_number = first_tile_own[:, None, None] + pair_index
    local_number = tile_number - first_tile_own[0]
    got_slot = tile_number % gx_count * slot_cap + local_number // gx_count
    both_alive = alive[:, :, None] & alive[:, None, :]
    matrix_mode = both_alive.astype(jnp.int32)
    matrix_from = jnp.where(both_alive, jnp.clip(got_slot, 0, slot_count - 1), 0)
    matrices = matrix_tiles(
        jnp.stack([matrix_from.reshape(-1), matrix_mode.reshape(-1)]), got_tiles, sub_count, NB
    )

    cases = residual.shape[1]
    cheb_center = (CHEB_HIGH + CHEB_LOW) / 2.0
    cheb_radius = (CHEB_HIGH - CHEB_LOW) / 2.0
    cheb_ratio = cheb_center / cheb_radius
    cheb_rho = 1.0 / cheb_ratio
    update = residual / cheb_center
    west_update = west_residual / cheb_center
    south_update = south_residual / cheb_center
    multipliers = jnp.zeros_like(residual)
    for sweep in range(ITERS):
        multipliers = multipliers + update
        east_part = update[..., : 2 * block_len]
        to_north_part = update[..., 2 * block_len :]
        west_in = -jnp.concatenate([west_update[None], east_part[: sub_count - 1]], axis=0)
        local_vec = jnp.concatenate([west_in, east_part, -south_update, to_north_part], axis=-1)
        high_f = lax.reduce_precision(local_vec, exponent_bits=8, mantissa_bits=7)
        high = high_f.astype(jnp.bfloat16)
        low = (local_vec - high_f).astype(jnp.bfloat16)
        both = jnp.einsum(
            "ncm,nmk->nck",
            jnp.concatenate([high, low], axis=1),
            matrices,
            preferred_element_type=jnp.float32,
        )
        image = both[:, :cases] + both[:, cases:]
        west_part = image[..., : 2 * block_len]
        split_east_part = image[..., 2 * block_len : 4 * block_len]
        south_part = image[..., 4 * block_len : 5 * block_len]
        split_north_part = image[..., 5 * block_len :]
        from_east = from_behind(west_part[0], "gx", -1)
        from_north = from_behind(south_part, "gy", -1)
        last = sweep == ITERS - 1
        if not last:
            west_east_part = from_behind(split_east_part[sub_count - 1], "gx", 1)
            south_north_part = from_behind(split_north_part, "gy", 1)
        east_near = jnp.concatenate([west_part[1:], from_east[None]], axis=0)
        residual = residual - jnp.concatenate(
            [split_east_part - east_near, split_north_part - from_north], axis=-1
        )
        rho_next = 1.0 / (2.0 * cheb_ratio - cheb_rho)
        keep = rho_next * cheb_rho
        step = 2.0 * rho_next / cheb_radius
        update = keep * update + step * residual
        if not last:
            west_residual = west_residual - (west_east_part - west_part[0])
            south_residual = south_residual - (south_north_part - south_part)
            west_update = keep * west_update + step * west_residual
            south_update = keep * south_update + step * south_residual
        cheb_rho = rho_next
    return (multipliers[:, None], residual[:, None])


def solution(mesh):
    in_specs = (
        P(None, "gy"),
        P("gx", "gy"),
        P("gx", "gy", None, None, None),
        P("gx", "gy", None, None),
    )
    out_specs = (P("gx", "gy", None, None), P("gx", "gy", None, None))
    return jax.shard_map(shards, mesh=mesh, in_specs=in_specs, out_specs=out_specs, check_vma=False)
```

```python
from functools import partial

import jax
import jax.numpy as jnp
from jax import lax
from jax.experimental import pallas as pl
from jax.experimental.pallas import tpu as pltpu
from jax.sharding import PartitionSpec as P

NB = 6
ITERS = 4


CHEB_LOW = 0.2
CHEB_HIGH = 7.0


def from_behind(value, axis, steps):
    count = lax.axis_size(axis)
    initial, last = (max(0, -steps), min(count, count - steps))
    return lax.ppermute(value, axis, [(source, source + steps) for source in range(initial, last)])


def _pack_kernel(code_ref, tiles_ref, out_ref, *, per_owner, owner_subs, block_len):
    out_ref[...] = jnp.zeros_like(out_ref)
    previous = jnp.int32(-1)
    rank = jnp.int32(0)
    for j in range(tiles_ref.shape[0]):
        code = code_ref[j]
        owner = lax.div(jnp.maximum(code, 0), jnp.int32(NB * NB * owner_subs))
        rank = jnp.where(owner == previous, rank + 1, 0)
        previous = owner
        slot = owner * per_owner + rank

        @pl.when((code >= 0) & (rank < per_owner))
        def _():
            out_ref[pl.ds(pl.multiple_of(slot * block_len, block_len), block_len), :] = tiles_ref[j]


def pack_tiles(codes, tiles, owners, per_owner, owner_subs):
    block_len = tiles.shape[-1]
    rows = owners * per_owner
    size = 2 * block_len * block_len
    return pl.pallas_call(
        partial(_pack_kernel, per_owner=per_owner, owner_subs=owner_subs, block_len=block_len),
        out_shape=jax.ShapeDtypeStruct((rows * block_len, block_len), tiles.dtype),
        in_specs=[
            pl.BlockSpec(memory_space=pltpu.SMEM),
            pl.BlockSpec(memory_space=pltpu.VMEM),
        ],
        out_specs=pl.BlockSpec(memory_space=pltpu.VMEM),
        cost_estimate=pl.CostEstimate(
            flops=0, transcendentals=0, bytes_accessed=(tiles.shape[0] + rows) * size
        ),
    )(codes, tiles)


def _matrix_kernel(table_ref, tiles_ref, out_ref, *, subs, blocks, block_len):
    for s in range(subs):
        for p in range(blocks):
            for q in range(p, blocks):
                entry = (s * blocks + p) * blocks + q
                tile = tiles_ref[table_ref[0, entry]]
                keep = table_ref[1, entry] != 0
                tile = jnp.where(keep, tile, jnp.zeros_like(tile))
                out_ref[s, p * block_len : (p + 1) * block_len, q * block_len : (q + 1) * block_len] = tile
                if q > p:
                    out_ref[s, q * block_len : (q + 1) * block_len, p * block_len : (p + 1) * block_len] = (
                        tile.T
                    )


def matrix_tiles(table, tiles, subs, blocks):
    block_len = tiles.shape[-1]
    size = 2 * block_len * block_len
    width = blocks * block_len
    return pl.pallas_call(
        partial(_matrix_kernel, subs=subs, blocks=blocks, block_len=block_len),
        out_shape=jax.ShapeDtypeStruct((subs, width, width), tiles.dtype),
        in_specs=[
            pl.BlockSpec(memory_space=pltpu.SMEM),
            pl.BlockSpec(memory_space=pltpu.VMEM),
        ],
        out_specs=pl.BlockSpec(memory_space=pltpu.VMEM),
        cost_estimate=pl.CostEstimate(
            flops=0, transcendentals=0, bytes_accessed=(tiles.shape[0] + subs * blocks * blocks) * size
        ),
    )(table, tiles)


def face_mask(counts, block_len):
    east_lane = jnp.arange(2 * block_len, dtype=jnp.int32) // block_len
    east_ok = east_lane < counts[..., 1:2]
    north_ok = jnp.zeros((block_len,), jnp.int32) < counts[..., 3:4]
    return jnp.concatenate([east_ok, north_ok], axis=-1).astype(jnp.float32)


def logical_slots(counts):
    west_n = counts[:, 0:1]
    east_n = counts[:, 1:2]
    south_n = counts[:, 2:3]
    north_n = counts[:, 3:4]
    within = jnp.array([0, 1, 0, 1, 0, 0], jnp.int32)[None, :]
    zero = jnp.zeros_like(west_n)
    offsets = jnp.concatenate(
        [zero, zero, west_n, west_n, west_n + east_n, west_n + east_n + south_n], axis=1
    )
    limits = jnp.concatenate([west_n, west_n, east_n, east_n, south_n, north_n], axis=1)
    return offsets + within, within < limits


def shards(east_blocks, job_code, factor_panels, dual_rhs):
    gx_count = lax.axis_size("gx")
    gy_count = lax.axis_size("gy")
    gx_index = lax.axis_index("gx")
    gy_index = lax.axis_index("gy")
    block_len = factor_panels.shape[-1]
    sub_count = dual_rhs.shape[0]
    column = east_blocks[:, 0]
    west_column = jnp.concatenate([jnp.zeros((1,), jnp.int32), column[:-1]])
    south_one = (gy_index > 0).astype(jnp.int32)
    north_one = (gy_index < gy_count - 1).astype(jnp.int32)
    blocks_all = west_column + column + south_one + north_one
    tiles_all = blocks_all * (blocks_all + 1) // 2
    first_tile_all = jnp.cumsum(tiles_all) - tiles_all
    first_sub = gx_index * sub_count
    east_own = lax.dynamic_slice_in_dim(column, first_sub, sub_count)
    west_own = lax.dynamic_slice_in_dim(west_column, first_sub, sub_count)
    blocks_own = lax.dynamic_slice_in_dim(blocks_all, first_sub, sub_count)
    first_tile_own = lax.dynamic_slice_in_dim(first_tile_all, first_sub, sub_count)
    south_own = jnp.broadcast_to(south_one, (sub_count,))
    north_own = jnp.broadcast_to(north_one, (sub_count,))
    counts = jnp.stack([west_own, east_own, south_own, north_own], axis=-1)

    residual = dual_rhs[:, 0] * face_mask(counts, block_len)[:, None, :]
    west_residual = from_behind(residual[sub_count - 1, :, : 2 * block_len], "gx", 1)
    south_residual = from_behind(residual[..., 2 * block_len :], "gy", 1)

    tiles = jnp.einsum(
        "jka,jkb->jab",
        factor_panels[:, 0, 0],
        factor_panels[:, 0, 1],
        preferred_element_type=jnp.float32,
    ).astype(jnp.bfloat16)
    slot_cap = (sub_count * NB * (NB + 1) // 2 + gx_count - 1) // gx_count
    slot_count = gx_count * slot_cap
    send_tiles = pack_tiles(job_code[:, 0], tiles, gx_count, slot_cap, sub_count)
    send_tiles = send_tiles.reshape(gx_count, slot_cap * block_len, block_len)
    got_tiles = lax.all_to_all(send_tiles, "gx", split_axis=0, concat_axis=0, tiled=True)
    got_tiles = got_tiles.reshape(slot_count, block_len, block_len)

    source, alive = logical_slots(counts)
    row_slot = source[:, :, None]
    col_slot = source[:, None, :]
    low_slot = jnp.minimum(row_slot, col_slot)
    high_slot = jnp.maximum(row_slot, col_slot)
    nb = blocks_own[:, None, None]
    pair_index = low_slot * nb - low_slot * (low_slot - 1) // 2 + (high_slot - low_slot)
    tile_number = first_tile_own[:, None, None] + pair_index
    local_number = tile_number - first_tile_own[0]
    got_slot = tile_number % gx_count * slot_cap + local_number // gx_count
    both_alive = alive[:, :, None] & alive[:, None, :]
    matrix_mode = both_alive.astype(jnp.int32)
    matrix_from = jnp.where(both_alive, jnp.clip(got_slot, 0, slot_count - 1), 0)
    matrices = matrix_tiles(
        jnp.stack([matrix_from.reshape(-1), matrix_mode.reshape(-1)]), got_tiles, sub_count, NB
    )

    cases = residual.shape[1]
    cheb_center = (CHEB_HIGH + CHEB_LOW) / 2.0
    cheb_radius = (CHEB_HIGH - CHEB_LOW) / 2.0
    cheb_ratio = cheb_center / cheb_radius
    cheb_rho = 1.0 / cheb_ratio
    update = residual / cheb_center
    west_update = west_residual / cheb_center
    south_update = south_residual / cheb_center
    multipliers = jnp.zeros_like(residual)
    for sweep in range(ITERS):
        multipliers = multipliers + update
        east_part = update[..., : 2 * block_len]
        to_north_part = update[..., 2 * block_len :]
        west_in = -jnp.concatenate([west_update[None], east_part[: sub_count - 1]], axis=0)
        local_vec = jnp.concatenate([west_in, east_part, -south_update, to_north_part], axis=-1)
        high_f = lax.reduce_precision(local_vec, exponent_bits=8, mantissa_bits=7)
        high = high_f.astype(jnp.bfloat16)
        low = (local_vec - high_f).astype(jnp.bfloat16)
        both = jnp.einsum(
            "ncm,nmk->nck",
            jnp.concatenate([high, low], axis=1),
            matrices,
            preferred_element_type=jnp.float32,
        )
        image = both[:, :cases] + both[:, cases:]
        west_part = image[..., : 2 * block_len]
        split_east_part = image[..., 2 * block_len : 4 * block_len]
        south_part = image[..., 4 * block_len : 5 * block_len]
        split_north_part = image[..., 5 * block_len :]
        from_east = from_behind(west_part[0], "gx", -1)
        from_north = from_behind(south_part, "gy", -1)
        last = sweep == ITERS - 1
        if not last:
            west_east_part = from_behind(split_east_part[sub_count - 1], "gx", 1)
            south_north_part = from_behind(split_north_part, "gy", 1)
        east_near = jnp.concatenate([west_part[1:], from_east[None]], axis=0)
        residual = residual - jnp.concatenate(
            [split_east_part - east_near, split_north_part - from_north], axis=-1
        )
        rho_next = 1.0 / (2.0 * cheb_ratio - cheb_rho)
        keep = rho_next * cheb_rho
        step = 2.0 * rho_next / cheb_radius
        update = keep * update + step * residual
        if not last:
            west_residual = west_residual - (west_east_part - west_part[0])
            south_residual = south_residual - (south_north_part - south_part)
            west_update = keep * west_update + step * west_residual
            south_update = keep * south_update + step * south_residual
        cheb_rho = rho_next
    return (multipliers[:, None], residual[:, None])


def solution(mesh):
    in_specs = (
        P(None, "gy"),
        P("gx", "gy"),
        P("gx", "gy", None, None, None),
        P("gx", "gy", None, None),
    )
    out_specs = (P("gx", "gy", None, None), P("gx", "gy", None, None))
    return jax.shard_map(shards, mesh=mesh, in_specs=in_specs, out_specs=out_specs, check_vma=False)
```

```python
from functools import partial

import jax
import jax.numpy as jnp
from jax import lax
from jax.experimental import pallas as pl
from jax.experimental.pallas import tpu as pltpu
from jax.sharding import PartitionSpec as P

NB = 6
ITERS = 4


CHEB_LOW = 0.2
CHEB_HIGH = 7.0


def from_behind(value, axis, steps):
    count = lax.axis_size(axis)
    initial, last = (max(0, -steps), min(count, count - steps))
    return lax.ppermute(value, axis, [(source, source + steps) for source in range(initial, last)])


def _pack_kernel(code_ref, tiles_ref, out_ref, *, per_owner, owner_subs, block_len):
    previous = jnp.int32(-1)
    rank = jnp.int32(0)
    for j in range(tiles_ref.shape[0]):
        code = code_ref[j]
        owner = lax.div(jnp.maximum(code, 0), jnp.int32(NB * NB * owner_subs))
        rank = jnp.where(owner == previous, rank + 1, 0)
        previous = owner
        slot = owner * per_owner + rank

        @pl.when((code >= 0) & (rank < per_owner))
        def _():
            out_ref[pl.ds(pl.multiple_of(slot * block_len, block_len), block_len), :] = tiles_ref[j]


def pack_tiles(codes, tiles, owners, per_owner, owner_subs):
    block_len = tiles.shape[-1]
    rows = owners * per_owner
    size = 2 * block_len * block_len
    return pl.pallas_call(
        partial(_pack_kernel, per_owner=per_owner, owner_subs=owner_subs, block_len=block_len),
        out_shape=jax.ShapeDtypeStruct((rows * block_len, block_len), tiles.dtype),
        in_specs=[
            pl.BlockSpec(memory_space=pltpu.SMEM),
            pl.BlockSpec(memory_space=pltpu.VMEM),
        ],
        out_specs=pl.BlockSpec(memory_space=pltpu.VMEM),
        cost_estimate=pl.CostEstimate(
            flops=0, transcendentals=0, bytes_accessed=(tiles.shape[0] + rows) * size
        ),
    )(codes, tiles)


def _matrix_kernel(table_ref, tiles_ref, out_ref, *, subs, blocks, block_len):
    for s in range(subs):
        for p in range(blocks):
            for q in range(p, blocks):
                entry = (s * blocks + p) * blocks + q
                tile = tiles_ref[table_ref[0, entry]]
                keep = table_ref[1, entry] != 0
                tile = jnp.where(keep, tile, jnp.zeros_like(tile))
                out_ref[s, p * block_len : (p + 1) * block_len, q * block_len : (q + 1) * block_len] = tile
                if q > p:
                    out_ref[s, q * block_len : (q + 1) * block_len, p * block_len : (p + 1) * block_len] = (
                        tile.astype(jnp.float32).T.astype(tile.dtype)
                    )


def matrix_tiles(table, tiles, subs, blocks):
    block_len = tiles.shape[-1]
    size = 2 * block_len * block_len
    width = blocks * block_len
    return pl.pallas_call(
        partial(_matrix_kernel, subs=subs, blocks=blocks, block_len=block_len),
        out_shape=jax.ShapeDtypeStruct((subs, width, width), tiles.dtype),
        in_specs=[
            pl.BlockSpec(memory_space=pltpu.SMEM),
            pl.BlockSpec(memory_space=pltpu.VMEM),
        ],
        out_specs=pl.BlockSpec(memory_space=pltpu.VMEM),
        cost_estimate=pl.CostEstimate(
            flops=0, transcendentals=0, bytes_accessed=(tiles.shape[0] + subs * blocks * blocks) * size
        ),
    )(table, tiles)


def face_mask(counts, block_len):
    east_lane = jnp.arange(2 * block_len, dtype=jnp.int32) // block_len
    east_ok = east_lane < counts[..., 1:2]
    north_ok = jnp.zeros((block_len,), jnp.int32) < counts[..., 3:4]
    return jnp.concatenate([east_ok, north_ok], axis=-1).astype(jnp.float32)


def logical_slots(counts):
    west_n = counts[:, 0:1]
    east_n = counts[:, 1:2]
    south_n = counts[:, 2:3]
    north_n = counts[:, 3:4]
    within = jnp.array([0, 1, 0, 1, 0, 0], jnp.int32)[None, :]
    zero = jnp.zeros_like(west_n)
    offsets = jnp.concatenate(
        [zero, zero, west_n, west_n, west_n + east_n, west_n + east_n + south_n], axis=1
    )
    limits = jnp.concatenate([west_n, west_n, east_n, east_n, south_n, north_n], axis=1)
    return offsets + within, within < limits


def shards(east_blocks, job_code, factor_panels, dual_rhs):
    gx_count = lax.axis_size("gx")
    gy_count = lax.axis_size("gy")
    gx_index = lax.axis_index("gx")
    gy_index = lax.axis_index("gy")
    block_len = factor_panels.shape[-1]
    sub_count = dual_rhs.shape[0]
    column = east_blocks[:, 0]
    west_column = jnp.concatenate([jnp.zeros((1,), jnp.int32), column[:-1]])
    south_one = (gy_index > 0).astype(jnp.int32)
    north_one = (gy_index < gy_count - 1).astype(jnp.int32)
    blocks_all = west_column + column + south_one + north_one
    tiles_all = blocks_all * (blocks_all + 1) // 2
    first_tile_all = jnp.cumsum(tiles_all) - tiles_all
    first_sub = gx_index * sub_count
    east_own = lax.dynamic_slice_in_dim(column, first_sub, sub_count)
    west_own = lax.dynamic_slice_in_dim(west_column, first_sub, sub_count)
    blocks_own = lax.dynamic_slice_in_dim(blocks_all, first_sub, sub_count)
    first_tile_own = lax.dynamic_slice_in_dim(first_tile_all, first_sub, sub_count)
    south_own = jnp.broadcast_to(south_one, (sub_count,))
    north_own = jnp.broadcast_to(north_one, (sub_count,))
    counts = jnp.stack([west_own, east_own, south_own, north_own], axis=-1)

    residual = dual_rhs[:, 0] * face_mask(counts, block_len)[:, None, :]
    west_residual = from_behind(residual[sub_count - 1, :, : 2 * block_len], "gx", 1)
    south_residual = from_behind(residual[..., 2 * block_len :], "gy", 1)

    tiles = jnp.einsum(
        "jka,jkb->jab",
        factor_panels[:, 0, 0],
        factor_panels[:, 0, 1],
        preferred_element_type=jnp.float32,
    ).astype(jnp.bfloat16)
    slot_cap = (sub_count * NB * (NB + 1) // 2 + gx_count - 1) // gx_count
    slot_count = gx_count * slot_cap
    send_tiles = pack_tiles(job_code[:, 0], tiles, gx_count, slot_cap, sub_count)
    send_tiles = send_tiles.reshape(gx_count, slot_cap * block_len, block_len)
    got_tiles = lax.all_to_all(send_tiles, "gx", split_axis=0, concat_axis=0, tiled=True)
    got_tiles = got_tiles.reshape(slot_count, block_len, block_len)

    source, alive = logical_slots(counts)
    row_slot = source[:, :, None]
    col_slot = source[:, None, :]
    low_slot = jnp.minimum(row_slot, col_slot)
    high_slot = jnp.maximum(row_slot, col_slot)
    nb = blocks_own[:, None, None]
    pair_index = low_slot * nb - low_slot * (low_slot - 1) // 2 + (high_slot - low_slot)
    tile_number = first_tile_own[:, None, None] + pair_index
    local_number = tile_number - first_tile_own[0]
    got_slot = tile_number % gx_count * slot_cap + local_number // gx_count
    both_alive = alive[:, :, None] & alive[:, None, :]
    matrix_mode = both_alive.astype(jnp.int32)
    matrix_from = jnp.where(both_alive, jnp.clip(got_slot, 0, slot_count - 1), 0)
    matrices = matrix_tiles(
        jnp.stack([matrix_from.reshape(-1), matrix_mode.reshape(-1)]), got_tiles, sub_count, NB
    )

    cases = residual.shape[1]
    cheb_center = (CHEB_HIGH + CHEB_LOW) / 2.0
    cheb_radius = (CHEB_HIGH - CHEB_LOW) / 2.0
    cheb_ratio = cheb_center / cheb_radius
    cheb_rho = 1.0 / cheb_ratio
    update = residual / cheb_center
    west_update = west_residual / cheb_center
    south_update = south_residual / cheb_center
    multipliers = jnp.zeros_like(residual)
    for sweep in range(ITERS):
        multipliers = multipliers + update
        east_part = update[..., : 2 * block_len]
        to_north_part = update[..., 2 * block_len :]
        west_in = -jnp.concatenate([west_update[None], east_part[: sub_count - 1]], axis=0)
        local_vec = jnp.concatenate([west_in, east_part, -south_update, to_north_part], axis=-1)
        high_f = lax.reduce_precision(local_vec, exponent_bits=8, mantissa_bits=7)
        high = high_f.astype(jnp.bfloat16)
        low = (local_vec - high_f).astype(jnp.bfloat16)
        both = jnp.einsum(
            "ncm,nmk->nck",
            jnp.concatenate([high, low], axis=1),
            matrices,
            preferred_element_type=jnp.float32,
        )
        image = both[:, :cases] + both[:, cases:]
        west_part = image[..., : 2 * block_len]
        split_east_part = image[..., 2 * block_len : 4 * block_len]
        south_part = image[..., 4 * block_len : 5 * block_len]
        split_north_part = image[..., 5 * block_len :]
        from_east = from_behind(west_part[0], "gx", -1)
        from_north = from_behind(south_part, "gy", -1)
        last = sweep == ITERS - 1
        if not last:
            west_east_part = from_behind(split_east_part[sub_count - 1], "gx", 1)
            south_north_part = from_behind(split_north_part, "gy", 1)
        east_near = jnp.concatenate([west_part[1:], from_east[None]], axis=0)
        residual = residual - jnp.concatenate(
            [split_east_part - east_near, split_north_part - from_north], axis=-1
        )
        rho_next = 1.0 / (2.0 * cheb_ratio - cheb_rho)
        keep = rho_next * cheb_rho
        step = 2.0 * rho_next / cheb_radius
        update = keep * update + step * residual
        if not last:
            west_residual = west_residual - (west_east_part - west_part[0])
            south_residual = south_residual - (south_north_part - south_part)
            west_update = keep * west_update + step * west_residual
            south_update = keep * south_update + step * south_residual
        cheb_rho = rho_next
    return (multipliers[:, None], residual[:, None])


def solution(mesh):
    in_specs = (
        P(None, "gy"),
        P("gx", "gy"),
        P("gx", "gy", None, None, None),
        P("gx", "gy", None, None),
    )
    out_specs = (P("gx", "gy", None, None), P("gx", "gy", None, None))
    return jax.shard_map(shards, mesh=mesh, in_specs=in_specs, out_specs=out_specs, check_vma=False)
```
